32 devices in a mesh: section: 2 (over core), dp: 4 (over z), mp: 4 (over y, x).
Axes of the slice: x: 2, y: 2, z: 4, core: 2. Of those that a mesh axis runs over, the one named last changes fastest.
Arguments:
- tokens: bfloat16 [1024, 2048], P('dp', 'mp'), may hold values from -40 to 40
- norm_gain: float32 [2, 2048], P('section'), may hold values from 0.25 to 1.75
- in_proj: bfloat16 [2, 2048, 4672], P('section', None, 'mp'), may hold values from -0.125 to 0.125
- conv_weight: float32 [2, 4, 2560], P('section', None, 'mp'), may hold values from -3 to 3
- conv_bias: float32 [2, 2560], P('section', 'mp'), may hold values from -3 to 3
- step_bias: float32 [2, 64], P('section', 'mp'), may hold values from -6 to -2
- decay_rate: float32 [2, 64], P('section', 'mp'), may hold values from 1 to 16
- skip_gain: float32 [2, 64], P('section', 'mp'), may hold values from 0.5 to 1.5
- gate_gain: float32 [2, 2048], P('section', 'mp'), may hold values from 0.25 to 1.75
- out_proj: bfloat16 [2, 2048, 2048], P('section', 'mp'), may hold values from -0.1875 to 0.1875
- kept_state: bfloat16 [2, 64, 64, 2048], P('section', 'dp', 'mp'), may hold values from -2 to 2
- kept_conv: bfloat16 [2, 64, 3, 2560], P('section', 'dp', None, 'mp'), may hold values from -6 to 6
- doc_owner: int32 [64], replicated, may hold values from 0 to 3, as said below
- doc_slot: int32 [64], replicated, may hold values from 0 to 15, as said below
- window_start: int32 [64], P('dp'), may hold values from 0 to 1136, as said below
Outputs:
- layer_out: bfloat16 [2, 1024, 2048], P('section', 'dp', 'mp')
- new_state: bfloat16 [2, 64, 64, 2048], P('section', 'dp', 'mp')
- new_conv: bfloat16 [2, 64, 3, 2560], P('section', 'dp', None, 'mp')
The draws below stay inside these ranges and needn't reach their ends.
Inputs may be any that keep to these rules, and one draw needn't show every extreme that they name: `doc_owner`: receiver q's documents are q * 16 to q * 16 + 15; each owner serves a receiver none or exactly 4 of its documents, and each owner keeps exactly 16 documents' states. `doc_slot`: the documents of one owner have distinct slots. `window_start`: A multiple of 16; 0 marks a book's first window.
All inputs are finite; a program needn't handle non-finite values.
Results may differ from the reference program's by a relative error of at most 0.012.
Values may be sent and summed in bfloat16 or wider, within the bound.
No kernel may reach another device: no remote copies, remote signals or barrier semaphores. Data moves between devices by JAX's collectives and lax.ppermute only.
A program may use at most 64 MiB of HBM per device.

```python
import math
import jax
import jax.numpy as jnp
from jax import lax

D = 2048
HEADS = 64
HEAD_DIM = 32
STATE = 64
CONV = 4
WINDOW = 16
DOCS = 16
LAYERS = 2
INNER = 2048
BLOCK = 1168
CHANNELS = 640
CAPACITY = 4
SLOTS = 16
TOKENS = 1024
N_DP = 4
N_MP = 4


def routing_table(key):
    base = jax.random.fold_in(key, 41)
    key_list = jax.random.split(base, 5)
    group_count = DOCS // CAPACITY
    offsets = jax.random.permutation(key_list[0], N_DP)[:group_count]
    outer_perm = jax.random.permutation(key_list[1], N_DP)
    inner_perm = jax.random.permutation(key_list[2], N_DP)
    receivers = jnp.arange(N_DP)
    doc_order = jax.vmap(lambda receiver: jax.random.permutation(jax.random.fold_in(key_list[3], receiver), DOCS))(receivers)
    group_of = doc_order // CAPACITY
    owners = outer_perm[(inner_perm[receivers][:, None] + offsets[group_of]) % N_DP]
    slot_order = jax.vmap(lambda receiver: jax.random.permutation(jax.random.fold_in(key_list[4], receiver), DOCS))(receivers)
    slots = slot_order[owners, doc_order]
    return (owners.reshape(-1).astype(jnp.int32), slots.reshape(-1).astype(jnp.int32))


def draw_doc_owner(key, part):
    return routing_table(key)[0]


def draw_doc_slot(key, part):
    return routing_table(key)[1]


def draw_window_start(key, part):
    raw_pick = jax.random.randint(jax.random.fold_in(key, 43), (N_DP * DOCS,), -24, 72)
    picked = jnp.maximum(raw_pick, 0)
    order = jax.random.permutation(jax.random.fold_in(key, 44), N_DP * DOCS)
    picked = picked.at[order[0]].set(71)
    picked = picked.at[order[1]].set(0)
    return (picked * WINDOW).astype(jnp.int32)


def draw_tokens(key, part):
    key_list = jax.random.split(jax.random.fold_in(key, 47), 3)
    row_scale = jnp.exp(jax.random.uniform(key_list[0], (TOKENS, 1), jnp.float32, -1.15, 1.15))
    col_scale = jnp.exp(jax.random.uniform(key_list[1], (1, D), jnp.float32, -1.15, 1.15))
    base = jnp.clip(jax.random.normal(key_list[2], (TOKENS, D), jnp.float32), -4.0, 4.0)
    return (base * row_scale * col_scale).astype(jnp.bfloat16)


def strengthened(entries, rng, source, target, parts, factor):
    owner, partner = [(jnp.arange(entries.shape[dim]) // (entries.shape[dim] // parts)).reshape([-1 if axis == dim else 1 for axis in range(entries.ndim)]) for dim in (source, target)]
    chosen = jax.random.permutation(rng, parts)[partner]
    strong = (owner == chosen) | (owner == (partner + parts // 2) % parts)
    return jnp.where(strong, factor * entries, entries)


def block_scale(own_key, shape, cuts, low, top_value):
    loudness, own = 1.0, jax.random.fold_in(own_key, 6)
    for dim, shards_of in cuts:
        draws = jnp.exp(jax.random.uniform(jax.random.fold_in(own, dim), (shards_of,), jnp.float32, low / len(cuts), top_value / len(cuts)))
        loudness = loudness * jnp.repeat(draws, shape[dim] // shards_of).reshape([-1 if axis == dim else 1 for axis in range(len(shape))])
    return loudness


def gaussian(own_key, dims, scale, limit, cuts=(), held_as=jnp.bfloat16):
    array = jax.random.normal(own_key, dims, jnp.float32) * scale
    if len(cuts) > 0:
        array = block_scale(own_key, dims, cuts, -0.22, 0.18) * array
    return jnp.clip(array, min=-limit, max=limit).astype(held_as)


def heavy_noise(key, dims, width, reach, pieces, heavy, held_as=jnp.bfloat16):
    entries = width * jax.random.normal(key, dims, jnp.float32)
    if pieces:
        entries = entries * block_scale(key, dims, pieces, -0.22, 0.18)
    return jnp.clip(strengthened(entries, jax.random.fold_in(key, 3), *heavy), -reach, reach).astype(held_as)


def setup_inputs(seed: int = 0) -> dict:
    key_of = jax.random.split(jax.random.key(seed), 16)
    return {
        "tokens": draw_tokens(jax.random.fold_in(key_of[15], 71), 0),
        "norm_gain": jnp.clip(1.0 + 0.15 * jax.random.normal(key_of[1], (LAYERS, D), jnp.float32), 0.25, 1.75),
        "in_proj": gaussian(key_of[2], (LAYERS, D, N_MP * BLOCK), D ** -0.5, 0.125, ((0, 2), (2, 4))),
        "conv_weight": gaussian(key_of[3], (LAYERS, CONV, N_MP * CHANNELS), CONV ** -0.5, 3.0, ((0, 2), (2, 4)), jnp.float32),
        "conv_bias": gaussian(key_of[4], (LAYERS, N_MP * CHANNELS), 0.5, 3.0, ((0, 2), (1, 4)), jnp.float32),
        "step_bias": jnp.clip(-6.0 + 4.0 * jax.random.uniform(key_of[5], (LAYERS, HEADS), jnp.float32) ** block_scale(key_of[5], (LAYERS, HEADS), ((0, 2), (1, 4)), -0.2, 0.2), -6.0, -2.0),
        "decay_rate": jnp.clip(jnp.exp(math.log(16.0) - 2.7725887 * jax.random.uniform(key_of[6], (LAYERS, HEADS), jnp.float32) ** block_scale(key_of[6], (LAYERS, HEADS), ((0, 2), (1, 4)), -0.2, 0.2)), 1.0, 16.0),
        "skip_gain": jnp.clip(0.5 + 1.0 * jax.random.uniform(key_of[7], (LAYERS, HEADS), jnp.float32) ** block_scale(key_of[7], (LAYERS, HEADS), ((0, 2), (1, 4)), -0.2, 0.2), 0.5, 1.5),
        "gate_gain": jnp.clip(1.0 + 0.15 * jax.random.normal(key_of[8], (LAYERS, INNER), jnp.float32), 0.25, 1.75),
        "out_proj": heavy_noise(key_of[9], (LAYERS, INNER, D), INNER ** -0.5, 0.1875, ((0, 2), (1, 4)), (1, 2, 4, 2.0)),
        "kept_state": gaussian(key_of[10], (LAYERS, N_DP * SLOTS, HEADS, HEAD_DIM * STATE), 0.3, 2.0, ((0, 2), (1, 4), (2, 4))),
        "kept_conv": gaussian(key_of[11], (LAYERS, N_DP * SLOTS, CONV - 1, N_MP * CHANNELS), 1.0, 6.0, ((0, 2), (1, 4), (3, 4))),
        "doc_owner": draw_doc_owner(jax.random.fold_in(key_of[15], 71), 0),
        "doc_slot": draw_doc_slot(jax.random.fold_in(key_of[15], 71), 0),
        "window_start": draw_window_start(jax.random.fold_in(key_of[15], 71), 0),
    }


epsilon = 1e-05
highest = lax.Precision.HIGHEST

def row_norm(values, norm_scale):
    inv_rms = lax.rsqrt(lax.optimization_barrier(jnp.mean(values * values, axis=-1, keepdims=True)) + epsilon)
    return values * inv_rms * norm_scale

def mix_window(projected, conv_prev, state_prev, conv_kernel, conv_shift, step_shift, decay_speed, skip_weight, norm_scale, out_weight):
    doc_count = projected.shape[0]
    length = projected.shape[1]
    inner = norm_scale.shape[0]
    head_count = decay_speed.shape[0]
    head_dim = inner // head_count
    state_width = (projected.shape[2] - 2 * inner - head_count) // 2
    kernel_len = conv_kernel.shape[0]
    gate_cols = projected[:, :, :inner]
    mixed_in = projected[:, :, inner:2 * inner + 2 * state_width]
    step_raw = projected[:, :, 2 * inner + 2 * state_width:]
    padded = jnp.concatenate([conv_prev, mixed_in], axis=1)
    conv_out = jnp.zeros_like(mixed_in) + conv_shift
    for offset in range(kernel_len):
        conv_out = conv_out + conv_kernel[offset] * padded[:, offset:offset + length]
    activated = jax.nn.silu(conv_out)
    head_vals = activated[:, :, :inner].reshape(doc_count, length, head_count, head_dim)
    key_proj = activated[:, :, inner:inner + state_width]
    query_proj = activated[:, :, inner + state_width:]
    step_size = jax.nn.softplus(step_raw + step_shift)
    log_decay = -step_size * decay_speed
    cum_decay = jnp.cumsum(log_decay, axis=1)
    pair_decay = cum_decay[:, :, None, :] - cum_decay[:, None, :, :]
    positions = jnp.arange(length)
    causal = positions[:, None] >= positions[None, :]
    decay = jnp.exp(jnp.where(causal[None, :, :, None], pair_decay, -1e+30))
    scores = jnp.einsum('dtn,dsn->dts', query_proj, key_proj, precision=highest)
    weights = decay * scores[:, :, :, None] * step_size[:, None, :, :]
    mixed_out = jnp.einsum('dtsh,dshp->dthp', weights, head_vals, precision=highest)
    start_state = state_prev.reshape(doc_count, head_count, head_dim, state_width)
    carried = jnp.einsum('dtn,dhpn->dthp', query_proj, start_state, precision=highest)
    mixed_out = mixed_out + jnp.exp(cum_decay)[:, :, :, None] * carried
    mixed_out = mixed_out + skip_weight[None, None, :, None] * head_vals
    tail_weight = jnp.exp(cum_decay[:, -1:, :] - cum_decay) * step_size
    end_state = jnp.exp(cum_decay[:, -1, :])[:, :, None, None] * start_state
    end_state = end_state + jnp.einsum('dsh,dshp,dsn->dhpn', tail_weight, head_vals, key_proj, precision=highest)
    new_conv = mixed_in[:, length - (kernel_len - 1):].astype(jnp.bfloat16)
    gated = mixed_out.reshape(doc_count, length, inner) * jax.nn.silu(gate_cols)
    gnormed = row_norm(gated, norm_scale).astype(jnp.bfloat16)
    partial_value = jnp.dot(gnormed.reshape(doc_count * length, inner), out_weight, preferred_element_type=jnp.float32)
    end_rounded = end_state.reshape(doc_count, head_count, head_dim * state_width).astype(jnp.bfloat16)
    return (partial_value, end_rounded, new_conv)

def reference(tokens, norm_gain, in_proj, conv_weight, conv_bias, step_bias, decay_rate, skip_gain, gate_gain, out_proj, kept_state, kept_conv, doc_owner, doc_slot, window_start):
    total_docs = N_DP * DOCS
    heads_dev = HEADS // N_MP
    inner_dev = HEADS * HEAD_DIM // N_MP
    chans = inner_dev + 2 * STATE
    keep_flag = (window_start > 0).astype(jnp.float32)
    source_row = (doc_owner * SLOTS + doc_slot).astype(jnp.int32)
    hidden = tokens
    layer_outs, layer_states, layer_convs = ([], [], [])
    for layer in range(LAYERS):
        normed = row_norm(hidden.astype(jnp.float32), norm_gain[layer]).astype(jnp.bfloat16)
        projected = jnp.dot(normed, in_proj[layer], preferred_element_type=jnp.float32)
        projected = projected.reshape(total_docs, WINDOW, N_MP, -1)
        state0 = kept_state[layer][source_row].astype(jnp.float32) * keep_flag[:, None, None]
        conv0 = kept_conv[layer][source_row].astype(jnp.float32) * keep_flag[:, None, None]
        conv0 = conv0.reshape(total_docs, CONV - 1, N_MP, chans)
        kernel_all = conv_weight[layer].reshape(CONV, N_MP, chans)
        shift_all = conv_bias[layer].reshape(N_MP, chans)
        running = hidden.astype(jnp.float32)
        group_states, group_convs = ([], [])
        for group in range(N_MP):
            head_lo = group * heads_dev
            inner_lo = group * inner_dev
            partial_value, end_state, new_conv = mix_window(projected[:, :, group], conv0[:, :, group], state0[:, head_lo:head_lo + heads_dev], kernel_all[:, group], shift_all[group], step_bias[layer, head_lo:head_lo + heads_dev], decay_rate[layer, head_lo:head_lo + heads_dev], skip_gain[layer, head_lo:head_lo + heads_dev], gate_gain[layer, inner_lo:inner_lo + inner_dev], out_proj[layer, inner_lo:inner_lo + inner_dev])
            rounded = lax.optimization_barrier(partial_value.astype(jnp.bfloat16))
            running = running + rounded.astype(jnp.float32)
            group_states.append(end_state)
            group_convs.append(new_conv)
        hidden = running.astype(jnp.bfloat16)
        layer_outs.append(hidden)
        layer_states.append(jnp.concatenate(group_states, axis=1))
        layer_convs.append(jnp.concatenate(group_convs, axis=2))
    return (jnp.stack(layer_outs), jnp.stack(layer_states), jnp.stack(layer_convs))
```

```python
import jax
import jax.numpy as jnp
from jax import lax
from jax.sharding import PartitionSpec as P

epsilon = 1e-05
highest = lax.Precision.HIGHEST


def from_behind(value, axis, steps):
    count = lax.axis_size(axis)
    first, last = (max(0, -steps), min(count, count - steps))
    return lax.ppermute(value, axis, [(source, source + steps) for source in range(first, last)])


def row_norm(values, norm_scale):
    inv_rms = lax.rsqrt(jnp.mean(values * values, axis=-1, keepdims=True) + epsilon)
    return values * inv_rms * norm_scale


def mix_window(
    projected,
    conv_prev,
    state_prev,
    conv_kernel,
    conv_shift,
    step_shift,
    decay_speed,
    skip_weight,
    norm_scale,
    out_weight,
):
    doc_count = projected.shape[0]
    length = projected.shape[1]
    inner = norm_scale.shape[0]
    head_count = decay_speed.shape[0]
    head_dim = inner // head_count
    state_width = (projected.shape[2] - 2 * inner - head_count) // 2
    kernel_len = conv_kernel.shape[0]
    gate_cols = projected[:, :, :inner]
    mixed_in = projected[:, :, inner : 2 * inner + 2 * state_width]
    step_raw = projected[:, :, 2 * inner + 2 * state_width :]
    padded = jnp.concatenate([conv_prev, mixed_in], axis=1)
    conv_out = jnp.zeros_like(mixed_in) + conv_shift
    for offset in range(kernel_len):
        conv_out = conv_out + conv_kernel[offset] * padded[:, offset : offset + length]
    activated = jax.nn.silu(conv_out)
    head_vals = activated[:, :, :inner].reshape(doc_count, length, head_count, head_dim)
    key_proj = activated[:, :, inner : inner + state_width]
    query_proj = activated[:, :, inner + state_width :]
    step_size = jax.nn.softplus(step_raw + step_shift)
    log_decay = -step_size * decay_speed
    cum_decay = jnp.cumsum(log_decay, axis=1)
    pair_decay = cum_decay[:, :, None, :] - cum_decay[:, None, :, :]
    positions = jnp.arange(length)
    causal = positions[:, None] >= positions[None, :]
    decay = jnp.exp(jnp.where(causal[None, :, :, None], pair_decay, -1e30))
    scores = jnp.einsum("dtn,dsn->dts", query_proj, key_proj, precision=highest)
    weights = decay * scores[:, :, :, None] * step_size[:, None, :, :]
    mixed_out = jnp.einsum("dtsh,dshp->dthp", weights, head_vals, precision=highest)
    start_state = state_prev.reshape(doc_count, head_count, head_dim, state_width)
    carried = jnp.einsum("dtn,dhpn->dthp", query_proj, start_state, precision=highest)
    mixed_out = mixed_out + jnp.exp(cum_decay)[:, :, :, None] * carried
    mixed_out = mixed_out + skip_weight[None, None, :, None] * head_vals
    tail_weight = jnp.exp(cum_decay[:, -1:, :] - cum_decay) * step_size
    end_state = jnp.exp(cum_decay[:, -1, :])[:, :, None, None] * start_state
    end_state = end_state + jnp.einsum(
        "dsh,dshp,dsn->dhpn", tail_weight, head_vals, key_proj, precision=highest
    )
    new_conv = mixed_in[:, length - (kernel_len - 1) :].astype(jnp.bfloat16)
    gated = mixed_out.reshape(doc_count, length, inner) * jax.nn.silu(gate_cols)
    gnormed = row_norm(gated, norm_scale).astype(jnp.bfloat16)
    partial_value = jnp.dot(
        gnormed.reshape(doc_count * length, inner), out_weight, preferred_element_type=jnp.float32
    )
    end_rounded = end_state.reshape(doc_count, head_count, head_dim * state_width).astype(
        jnp.bfloat16
    )
    return (partial_value, end_rounded, new_conv)


def shifted(value, axis, steps):
    count = lax.axis_size(axis)
    return lax.ppermute(value, axis, [(source, (source + steps) % count) for source in range(count)])


def gather_columns(value):
    count = lax.axis_size("mp")
    width = value.shape[1]
    position = lax.axis_index("mp")
    parts = [value] + [shifted(value, "mp", steps) for steps in range(1, count)]
    joined = jnp.concatenate(parts[::-1], axis=1)
    doubled = jnp.concatenate([joined, joined], axis=1)
    return lax.dynamic_slice_in_dim(doubled, ((count - 1 - position) % count) * width, count * width, 1)


def scatter_sum(partial_value, base):
    count = lax.axis_size("mp")
    position = lax.axis_index("mp")
    rows = partial_value.shape[0]
    blocks = partial_value.astype(jnp.bfloat16).reshape(rows, count, -1)
    total = base + lax.dynamic_index_in_dim(blocks, position, 1, False).astype(jnp.float32)
    for steps in range(1, count):
        block = lax.dynamic_index_in_dim(blocks, (position + steps) % count, 1, False)
        total = total + shifted(block, "mp", steps).astype(jnp.float32)
    return total


def per_device(
    tokens,
    norm_gain,
    in_proj,
    conv_weight,
    conv_bias,
    step_bias,
    decay_rate,
    skip_gain,
    gate_gain,
    out_proj,
    kept_state,
    kept_conv,
    doc_owner,
    doc_slot,
    window_start,
):
    dp_count = lax.axis_size("dp")
    section_count = lax.axis_size("section")
    dp_idx = lax.axis_index("dp")
    section_idx = lax.axis_index("section")
    doc_count = window_start.shape[0]
    length = tokens.shape[0] // doc_count
    shard_width = tokens.shape[1]
    capacity = (doc_count + dp_count - 1) // dp_count
    owners = doc_owner.reshape(dp_count, doc_count)
    slots = doc_slot.reshape(dp_count, doc_count)
    positions = jnp.arange(doc_count)
    earlier = positions[:, None] > positions[None, :]
    same_owner = owners[:, :, None] == owners[:, None, :]
    owner_rank = jnp.sum(jnp.logical_and(same_owner, earlier[None]), axis=2)
    chosen = jnp.logical_and(
        (owners == dp_idx)[:, :, None],
        owner_rank[:, :, None] == jnp.arange(capacity)[None, None, :],
    )
    send_index = jnp.sum(jnp.where(chosen, slots[:, :, None], 0), axis=1).reshape(-1)
    heads_dev = kept_state.shape[2]
    state_cols = kept_state.shape[3]
    chans = conv_weight.shape[2]
    kernel_len = conv_weight.shape[1]
    send_state = kept_state[0][send_index].reshape(send_index.shape[0], -1)
    send_conv = kept_conv[0][send_index].reshape(send_index.shape[0], -1)
    state_size = send_state.shape[1]
    got_both = lax.all_to_all(
        jnp.concatenate([send_state, send_conv], axis=1), "dp", split_axis=0, concat_axis=0, tiled=True
    )
    my_owners = lax.dynamic_index_in_dim(owners, dp_idx, 0, keepdims=False)
    my_rank = lax.dynamic_index_in_dim(owner_rank, dp_idx, 0, keepdims=False)
    recv_row = my_owners * capacity + my_rank
    keep_flag = (window_start > 0).astype(jnp.float32)
    got_rows = got_both[recv_row].astype(jnp.float32) * keep_flag[:, None]
    state_start = got_rows[:, :state_size].reshape(doc_count, heads_dev, state_cols)
    conv_start = got_rows[:, state_size:].reshape(doc_count, kernel_len - 1, chans)
    group_docs = 4
    block_count = doc_count // group_docs
    block_rows = group_docs * length
    tick_count = block_count + section_count - 1

    incoming = jnp.zeros((block_rows, shard_width), jnp.bfloat16)
    results, states, convs = [], [], []
    for tick_idx in range(tick_count):
        block_idx = jnp.clip(tick_idx - section_idx, 0, block_count - 1)
        first_rows = tokens[min(tick_idx, block_count - 1) * block_rows :][:block_rows]
        current = jnp.where(section_idx == 0, first_rows, incoming)
        whole_rows = gather_columns(current)
        normed = row_norm(whole_rows.astype(jnp.float32), norm_gain[0]).astype(jnp.bfloat16)
        projected = jnp.dot(normed, in_proj[0], preferred_element_type=jnp.float32)
        conv_prev = lax.dynamic_slice_in_dim(conv_start, block_idx * group_docs, group_docs, 0)
        state_prev = lax.dynamic_slice_in_dim(state_start, block_idx * group_docs, group_docs, 0)
        partial_value, state_new, conv_new = mix_window(
            projected.reshape(group_docs, length, -1),
            conv_prev,
            state_prev,
            conv_weight[0],
            conv_bias[0],
            step_bias[0],
            decay_rate[0],
            skip_gain[0],
            gate_gain[0],
            out_proj[0],
        )
        result = scatter_sum(partial_value, current.astype(jnp.float32)).astype(jnp.bfloat16)
        results.append(result)
        states.append(state_new)
        convs.append(conv_new)
        if tick_idx + 1 < tick_count:
            incoming = from_behind(result, "section", 1)

    def pick(items, offset):
        return jnp.concatenate(items[offset : offset + block_count], axis=0)

    first = section_idx == 0
    out_rows = jnp.where(first, pick(results, 0), pick(results, section_count - 1))
    new_states = jnp.where(first, pick(states, 0), pick(states, section_count - 1))
    new_convs = jnp.where(first, pick(convs, 0), pick(convs, section_count - 1))
    return (out_rows[None], new_states[None], new_convs[None])


def solution(mesh):
    in_specs = (
        P("dp", "mp"),
        P("section", None),
        P("section", None, "mp"),
        P("section", None, "mp"),
        P("section", "mp"),
        P("section", "mp"),
        P("section", "mp"),
        P("section", "mp"),
        P("section", "mp"),
        P("section", "mp", None),
        P("section", "dp", "mp", None),
        P("section", "dp", None, "mp"),
        P(),
        P(),
        P("dp"),
    )
    out_specs = (
        P("section", "dp", "mp"),
        P("section", "dp", "mp", None),
        P("section", "dp", None, "mp"),
    )
    return jax.shard_map(
        per_device, mesh=mesh, in_specs=in_specs, out_specs=out_specs, check_vma=False
    )
```

```python
import jax
import jax.numpy as jnp
from jax import lax
from jax.sharding import PartitionSpec as P

epsilon = 1e-05
highest = lax.Precision.HIGHEST


def from_behind(value, axis, steps):
    count = lax.axis_size(axis)
    first, last = (max(0, -steps), min(count, count - steps))
    return lax.ppermute(value, axis, [(source, source + steps) for source in range(first, last)])


def row_norm(values, norm_scale):
    inv_rms = lax.rsqrt(jnp.mean(values * values, axis=-1, keepdims=True) + epsilon)
    return values * inv_rms * norm_scale


def mix_channels(
    projected,
    conv_prev,
    state_prev,
    conv_kernel,
    conv_shift,
    step_shift,
    decay_speed,
    skip_weight,
    norm_scale,
    out_weight,
):
    doc_count = projected.shape[0]
    length = projected.shape[1]
    inner = norm_scale.shape[0]
    head_count = decay_speed.shape[0]
    head_dim = inner // head_count
    state_width = (projected.shape[2] - 2 * inner - head_count) // 2
    kernel_len = conv_kernel.shape[0]
    gate_cols = projected[:, :, :inner]
    mixed_in = projected[:, :, inner : 2 * inner + 2 * state_width]
    step_raw = projected[:, :, 2 * inner + 2 * state_width :]
    padded = jnp.concatenate([conv_prev, mixed_in], axis=1)
    conv_out = jnp.zeros_like(mixed_in) + conv_shift
    for offset in range(kernel_len):
        conv_out = conv_out + conv_kernel[offset] * padded[:, offset : offset + length]
    activated = jax.nn.silu(conv_out)
    chan_vals = activated[:, :, :inner]
    key_proj = activated[:, :, inner : inner + state_width]
    query_proj = activated[:, :, inner + state_width :]
    step_size = jax.nn.softplus(step_raw + step_shift)
    cum_decay = jnp.cumsum(-step_size * decay_speed, axis=1)
    pair_decay = cum_decay[:, :, None, :] - cum_decay[:, None, :, :]
    positions = jnp.arange(length)
    causal = positions[:, None] >= positions[None, :]
    decay = jnp.exp(jnp.where(causal[None, :, :, None], pair_decay, -1e30))
    scores = jnp.einsum("dtn,dsn->dts", query_proj, key_proj, precision=highest)
    weights = decay * scores[:, :, :, None] * step_size[:, None, :, :]
    chan_weights = jnp.repeat(weights, head_dim, axis=3)
    mixed_out = jnp.sum(chan_weights * chan_vals[:, None, :, :], axis=2)
    start_state = state_prev.reshape(doc_count, inner, state_width).astype(jnp.float32)
    carried = jnp.einsum("dtn,dmn->dtm", query_proj, start_state, precision=highest)
    mixed_out = mixed_out + jnp.repeat(jnp.exp(cum_decay), head_dim, axis=2) * carried
    mixed_out = mixed_out + jnp.repeat(skip_weight, head_dim)[None, None, :] * chan_vals
    tail_weight = jnp.exp(cum_decay[:, -1:, :] - cum_decay) * step_size
    scaled_vals = jnp.repeat(tail_weight, head_dim, axis=2) * chan_vals
    end_state = jnp.repeat(jnp.exp(cum_decay[:, -1, :]), head_dim, axis=1)[:, :, None] * start_state
    end_state = end_state + jnp.einsum("dsm,dsn->dmn", scaled_vals, key_proj, precision=highest)
    new_conv = mixed_in[:, length - (kernel_len - 1) :].astype(jnp.bfloat16)
    gated = mixed_out * jax.nn.silu(gate_cols)
    gnormed = row_norm(gated, norm_scale).astype(jnp.bfloat16)
    partial_value = jnp.dot(
        gnormed.reshape(doc_count * length, inner), out_weight, preferred_element_type=jnp.float32
    )
    end_rounded = end_state.reshape(doc_count, head_count, head_dim * state_width).astype(
        jnp.bfloat16
    )
    return (partial_value, end_rounded, new_conv)


def shifted(value, axis, steps):
    count = lax.axis_size(axis)
    return lax.ppermute(value, axis, [(source, (source + steps) % count) for source in range(count)])


def gather_columns(value):
    count = lax.axis_size("mp")
    width = value.shape[1]
    position = lax.axis_index("mp")
    parts = [value] + [shifted(value, "mp", steps) for steps in range(1, count)]
    joined = jnp.concatenate(parts[::-1], axis=1)
    doubled = jnp.concatenate([joined, joined], axis=1)
    return lax.dynamic_slice_in_dim(doubled, ((count - 1 - position) % count) * width, count * width, 1)


def scatter_sum(partial_value, base):
    count = lax.axis_size("mp")
    position = lax.axis_index("mp")
    rows = partial_value.shape[0]
    blocks = partial_value.astype(jnp.bfloat16).reshape(rows, count, -1)
    total = base + lax.dynamic_index_in_dim(blocks, position, 1, False).astype(jnp.float32)
    for steps in range(1, count):
        block = lax.dynamic_index_in_dim(blocks, (position + steps) % count, 1, False)
        total = total + shifted(block, "mp", steps).astype(jnp.float32)
    return total


def per_device(
    tokens,
    norm_gain,
    in_proj,
    conv_weight,
    conv_bias,
    step_bias,
    decay_rate,
    skip_gain,
    gate_gain,
    out_proj,
    kept_state,
    kept_conv,
    doc_owner,
    doc_slot,
    window_start,
):
    dp_count = lax.axis_size("dp")
    section_count = lax.axis_size("section")
    dp_idx = lax.axis_index("dp")
    section_idx = lax.axis_index("section")
    doc_count = window_start.shape[0]
    length = tokens.shape[0] // doc_count
    shard_width = tokens.shape[1]
    capacity = (doc_count + dp_count - 1) // dp_count
    owners = doc_owner.reshape(dp_count, doc_count)
    slots = doc_slot.reshape(dp_count, doc_count)
    positions = jnp.arange(doc_count)
    earlier = positions[:, None] > positions[None, :]
    same_owner = owners[:, :, None] == owners[:, None, :]
    owner_rank = jnp.sum(jnp.logical_and(same_owner, earlier[None]), axis=2)
    chosen = jnp.logical_and(
        (owners == dp_idx)[:, :, None],
        owner_rank[:, :, None] == jnp.arange(capacity)[None, None, :],
    )
    send_index = jnp.sum(jnp.where(chosen, slots[:, :, None], 0), axis=1).reshape(-1)
    heads_dev = kept_state.shape[2]
    state_cols = kept_state.shape[3]
    chans = conv_weight.shape[2]
    kernel_len = conv_weight.shape[1]
    send_state = kept_state[0][send_index].reshape(send_index.shape[0], -1)
    send_conv = kept_conv[0][send_index].reshape(send_index.shape[0], -1)
    state_size = send_state.shape[1]
    got_both = lax.all_to_all(
        jnp.concatenate([send_state, send_conv], axis=1), "dp", split_axis=0, concat_axis=0, tiled=True
    )
    my_owners = lax.dynamic_index_in_dim(owners, dp_idx, 0, keepdims=False)
    my_rank = lax.dynamic_index_in_dim(owner_rank, dp_idx, 0, keepdims=False)
    recv_row = my_owners * capacity + my_rank
    keep_flag = (window_start > 0).astype(jnp.float32)
    got_rows = got_both[recv_row].astype(jnp.float32) * keep_flag[:, None]
    state_start = got_rows[:, :state_size].reshape(doc_count, heads_dev, state_cols)
    conv_start = got_rows[:, state_size:].reshape(doc_count, kernel_len - 1, chans)
    results = None
    incoming = None
    for phase in range(section_count):
        if incoming is None:
            current = tokens
        else:
            current = jnp.where(section_idx == 0, tokens, incoming)
        whole_rows = gather_columns(current)
        normed = row_norm(whole_rows.astype(jnp.float32), norm_gain[0]).astype(jnp.bfloat16)
        projected = jnp.dot(normed, in_proj[0], preferred_element_type=jnp.float32)
        partial_value, state_new, conv_new = mix_channels(
            projected.reshape(doc_count, length, -1),
            conv_start,
            state_start,
            conv_weight[0],
            conv_bias[0],
            step_bias[0],
            decay_rate[0],
            skip_gain[0],
            gate_gain[0],
            out_proj[0],
        )
        result = scatter_sum(partial_value, current.astype(jnp.float32)).astype(jnp.bfloat16)
        results = (result, state_new, conv_new)
        if phase + 1 < section_count:
            incoming = from_behind(result, "section", 1)
    out_rows, new_states, new_convs = results
    return (out_rows[None], new_states[None], new_convs[None])


def solution(mesh):
    in_specs = (
        P("dp", "mp"),
        P("section", None),
        P("section", None, "mp"),
        P("section", None, "mp"),
        P("section", "mp"),
        P("section", "mp"),
        P("section", "mp"),
        P("section", "mp"),
        P("section", "mp"),
        P("section", "mp", None),
        P("section", "dp", "mp", None),
        P("section", "dp", None, "mp"),
        P(),
        P(),
        P("dp"),
    )
    out_specs = (
        P("section", "dp", "mp"),
        P("section", "dp", "mp", None),
        P("section", "dp", None, "mp"),
    )
    return jax.shard_map(
        per_device, mesh=mesh, in_specs=in_specs, out_specs=out_specs, check_vma=False
    )
```

```python
import jax
import jax.numpy as jnp
from jax import lax
from jax.sharding import PartitionSpec as P

epsilon = 1e-05
highest = lax.Precision.HIGHEST


def from_behind(value, axis, steps):
    count = lax.axis_size(axis)
    first, last = (max(0, -steps), min(count, count - steps))
    return lax.ppermute(value, axis, [(source, source + steps) for source in range(first, last)])


def row_norm(values, norm_scale):
    inv_rms = lax.rsqrt(jnp.mean(values * values, axis=-1, keepdims=True) + epsilon)
    return values * inv_rms * norm_scale


def mix_channels(
    projected,
    conv_prev,
    state_prev,
    conv_kernel,
    conv_shift,
    step_shift,
    decay_speed,
    skip_weight,
    norm_scale,
    out_weight,
):
    doc_count = projected.shape[0]
    length = projected.shape[1]
    inner = norm_scale.shape[0]
    head_count = decay_speed.shape[0]
    head_dim = inner // head_count
    state_width = (projected.shape[2] - 2 * inner - head_count) // 2
    kernel_len = conv_kernel.shape[0]
    gate_cols = projected[:, :, :inner]
    mixed_in = projected[:, :, inner : 2 * inner + 2 * state_width]
    step_raw = projected[:, :, 2 * inner + 2 * state_width :]
    padded = jnp.concatenate([conv_prev, mixed_in], axis=1)
    conv_out = jnp.zeros_like(mixed_in) + conv_shift
    for offset in range(kernel_len):
        conv_out = conv_out + conv_kernel[offset] * padded[:, offset : offset + length]
    activated = jax.nn.silu(conv_out)
    chan_vals = activated[:, :, :inner]
    expander = (
        jnp.arange(inner)[None, :] // head_dim == jnp.arange(head_count)[:, None]
    ).astype(jnp.float32)

    def expand(per_head):
        return jnp.einsum("...h,hm->...m", per_head, expander, precision=highest)

    key_proj = activated[:, :, inner : inner + state_width]
    query_proj = activated[:, :, inner + state_width :]
    step_size = jax.nn.softplus(step_raw + step_shift)
    cum_decay = jnp.cumsum(-step_size * decay_speed, axis=1)
    pair_decay = cum_decay[:, :, None, :] - cum_decay[:, None, :, :]
    positions = jnp.arange(length)
    causal = positions[:, None] >= positions[None, :]
    decay = jnp.exp(jnp.where(causal[None, :, :, None], pair_decay, -1e30))
    scores = jnp.einsum("dtn,dsn->dts", query_proj, key_proj, precision=highest)
    weights = decay * scores[:, :, :, None] * step_size[:, None, :, :]
    chan_weights = jnp.repeat(weights, head_dim, axis=3)
    mixed_out = jnp.sum(chan_weights * chan_vals[:, None, :, :], axis=2)
    start_state = state_prev.reshape(doc_count, inner, state_width).astype(jnp.float32)
    carried = jnp.einsum("dtn,dmn->dtm", query_proj, start_state, precision=highest)
    mixed_out = mixed_out + expand(jnp.exp(cum_decay)) * carried
    mixed_out = mixed_out + jnp.repeat(skip_weight, head_dim)[None, None, :] * chan_vals
    tail_weight = jnp.exp(cum_decay[:, -1:, :] - cum_decay) * step_size
    scaled_vals = expand(tail_weight) * chan_vals
    end_state = expand(jnp.exp(cum_decay[:, -1, :]))[:, :, None] * start_state
    end_state = end_state + jnp.einsum("dsm,dsn->dmn", scaled_vals, key_proj, precision=highest)
    new_conv = mixed_in[:, length - (kernel_len - 1) :].astype(jnp.bfloat16)
    gated = mixed_out * jax.nn.silu(gate_cols)
    gnormed = row_norm(gated, norm_scale).astype(jnp.bfloat16)
    partial_value = jnp.dot(
        gnormed.reshape(doc_count * length, inner), out_weight, preferred_element_type=jnp.float32
    )
    end_rounded = end_state.reshape(doc_count, head_count, head_dim * state_width).astype(
        jnp.bfloat16
    )
    return (partial_value, end_rounded, new_conv)


def shifted(value, axis, steps):
    count = lax.axis_size(axis)
    return lax.ppermute(value, axis, [(source, (source + steps) % count) for source in range(count)])


def gather_columns(value):
    count = lax.axis_size("mp")
    width = value.shape[1]
    position = lax.axis_index("mp")
    parts = [value] + [shifted(value, "mp", steps) for steps in range(1, count)]
    joined = jnp.concatenate(parts[::-1], axis=1)
    doubled = jnp.concatenate([joined, joined], axis=1)
    return lax.dynamic_slice_in_dim(doubled, ((count - 1 - position) % count) * width, count * width, 1)


def gather_from_behind(value):
    count = lax.axis_size("mp")
    sections = lax.axis_size("section")
    width = value.shape[1]
    position = lax.axis_index("mp")
    parts = []
    for steps in range(count):
        pairs = [
            (section * count + source, (section + 1) * count + (source + steps) % count)
            for section in range(sections - 1)
            for source in range(count)
        ]
        parts.append(lax.ppermute(value, ("section", "mp"), pairs))
    joined = jnp.concatenate(parts[::-1], axis=1)
    doubled = jnp.concatenate([joined, joined], axis=1)
    whole = lax.dynamic_slice_in_dim(doubled, ((count - 1 - position) % count) * width, count * width, 1)
    return whole, parts[0]


def scatter_sum(partial_value, base):
    count = lax.axis_size("mp")
    position = lax.axis_index("mp")
    rows = partial_value.shape[0]
    blocks = partial_value.astype(jnp.bfloat16).reshape(rows, count, -1)
    total = base + lax.dynamic_index_in_dim(blocks, position, 1, False).astype(jnp.float32)
    for steps in range(1, count):
        block = lax.dynamic_index_in_dim(blocks, (position + steps) % count, 1, False)
        total = total + shifted(block, "mp", steps).astype(jnp.float32)
    return total


def per_device(
    tokens,
    norm_gain,
    in_proj,
    conv_weight,
    conv_bias,
    step_bias,
    decay_rate,
    skip_gain,
    gate_gain,
    out_proj,
    kept_state,
    kept_conv,
    doc_owner,
    doc_slot,
    window_start,
):
    dp_count = lax.axis_size("dp")
    section_count = lax.axis_size("section")
    dp_idx = lax.axis_index("dp")
    section_idx = lax.axis_index("section")
    doc_count = window_start.shape[0]
    length = tokens.shape[0] // doc_count
    shard_width = tokens.shape[1]
    capacity = (doc_count + dp_count - 1) // dp_count
    owners = doc_owner.reshape(dp_count, doc_count)
    slots = doc_slot.reshape(dp_count, doc_count)
    positions = jnp.arange(doc_count)
    earlier = positions[:, None] > positions[None, :]
    same_owner = owners[:, :, None] == owners[:, None, :]
    owner_rank = jnp.sum(jnp.logical_and(same_owner, earlier[None]), axis=2)
    chosen = jnp.logical_and(
        (owners == dp_idx)[:, :, None],
        owner_rank[:, :, None] == jnp.arange(capacity)[None, None, :],
    )
    send_index = jnp.sum(jnp.where(chosen, slots[:, :, None], 0), axis=1).reshape(-1)
    heads_dev = kept_state.shape[2]
    state_cols = kept_state.shape[3]
    chans = conv_weight.shape[2]
    kernel_len = conv_weight.shape[1]
    send_state = kept_state[0][send_index].reshape(send_index.shape[0], -1)
    send_conv = kept_conv[0][send_index].reshape(send_index.shape[0], -1)
    state_size = send_state.shape[1]
    got_both = lax.all_to_all(
        jnp.concatenate([send_state, send_conv], axis=1), "dp", split_axis=0, concat_axis=0, tiled=True
    )
    my_owners = lax.dynamic_index_in_dim(owners, dp_idx, 0, keepdims=False)
    my_rank = lax.dynamic_index_in_dim(owner_rank, dp_idx, 0, keepdims=False)
    recv_row = my_owners * capacity + my_rank
    keep_flag = (window_start > 0).astype(jnp.float32)
    got_rows = got_both[recv_row].astype(jnp.float32) * keep_flag[:, None]
    state_start = got_rows[:, :state_size].reshape(doc_count, heads_dev, state_cols)
    conv_start = got_rows[:, state_size:].reshape(doc_count, kernel_len - 1, chans)
    results = None
    incoming = None
    first_rows = None
    for phase in range(section_count):
        if incoming is None:
            current = tokens
            whole_rows = gather_columns(current)
            first_rows = whole_rows
        else:
            gathered, incoming = gather_from_behind(result)
            current = jnp.where(section_idx == 0, tokens, incoming)
            whole_rows = jnp.where(section_idx == 0, first_rows, gathered)
        normed = row_norm(whole_rows.astype(jnp.float32), norm_gain[0]).astype(jnp.bfloat16)
        projected = jnp.dot(normed, in_proj[0], preferred_element_type=jnp.float32)
        partial_value, state_new, conv_new = mix_channels(
            projected.reshape(doc_count, length, -1),
            conv_start,
            state_start,
            conv_weight[0],
            conv_bias[0],
            step_bias[0],
            decay_rate[0],
            skip_gain[0],
            gate_gain[0],
            out_proj[0],
        )
        result = scatter_sum(partial_value, current.astype(jnp.float32)).astype(jnp.bfloat16)
        results = (result, state_new, conv_new)
        incoming = result
    out_rows, new_states, new_convs = results
    return (out_rows[None], new_states[None], new_convs[None])


def solution(mesh):
    in_specs = (
        P("dp", "mp"),
        P("section", None),
        P("section", None, "mp"),
        P("section", None, "mp"),
        P("section", "mp"),
        P("section", "mp"),
        P("section", "mp"),
        P("section", "mp"),
        P("section", "mp"),
        P("section", "mp", None),
        P("section", "dp", "mp", None),
        P("section", "dp", None, "mp"),
        P(),
        P(),
        P("dp"),
    )
    out_specs = (
        P("section", "dp", "mp"),
        P("section", "dp", "mp", None),
        P("section", "dp", None, "mp"),
    )
    return jax.shard_map(
        per_device, mesh=mesh, in_specs=in_specs, out_specs=out_specs, check_vma=False
    )
```

```python
import jax
import jax.numpy as jnp
from jax import lax
from jax.sharding import PartitionSpec as P

epsilon = 1e-05
highest = lax.Precision.HIGHEST


def from_behind(value, axis, steps):
    count = lax.axis_size(axis)
    first, last = (max(0, -steps), min(count, count - steps))
    return lax.ppermute(value, axis, [(source, source + steps) for source in range(first, last)])


def row_norm(values, norm_scale):
    inv_rms = lax.rsqrt(jnp.mean(values * values, axis=-1, keepdims=True) + epsilon)
    return values * inv_rms * norm_scale


def mix_channels(
    projected,
    conv_prev,
    state_prev,
    conv_kernel,
    conv_shift,
    step_shift,
    decay_speed,
    skip_weight,
    norm_scale,
    out_weight,
):
    doc_count = projected.shape[0]
    length = projected.shape[1]
    inner = norm_scale.shape[0]
    head_count = decay_speed.shape[0]
    head_dim = inner // head_count
    state_width = (projected.shape[2] - 2 * inner - head_count) // 2
    kernel_len = conv_kernel.shape[0]
    gate_cols = projected[:, :, :inner]
    mixed_in = projected[:, :, inner : 2 * inner + 2 * state_width]
    step_raw = projected[:, :, 2 * inner + 2 * state_width :]
    padded = jnp.concatenate([conv_prev, mixed_in], axis=1)
    conv_out = jnp.zeros_like(mixed_in) + conv_shift
    for offset in range(kernel_len):
        conv_out = conv_out + conv_kernel[offset] * padded[:, offset : offset + length]
    activated = jax.nn.silu(conv_out)
    chan_vals = activated[:, :, :inner]
    expander = (
        jnp.arange(inner)[None, :] // head_dim == jnp.arange(head_count)[:, None]
    ).astype(jnp.float32)

    def expand(per_head):
        return jnp.einsum("...h,hm->...m", per_head, expander, precision=highest)

    key_proj = activated[:, :, inner : inner + state_width]
    query_proj = activated[:, :, inner + state_width :]
    step_size = jax.nn.softplus(step_raw + step_shift)
    cum_decay = jnp.cumsum(-step_size * decay_speed, axis=1)
    pair_decay = cum_decay[:, :, None, :] - cum_decay[:, None, :, :]
    positions = jnp.arange(length)
    causal = positions[:, None] >= positions[None, :]
    decay = jnp.exp(jnp.where(causal[None, :, :, None], pair_decay, -1e30))
    scores = jnp.einsum("dtn,dsn->dts", query_proj, key_proj, precision=highest)
    weights = decay * scores[:, :, :, None] * step_size[:, None, :, :]
    spread = chan_vals[:, :, None, :] * expander[None, None, :, :]
    mixed_out = jnp.einsum("dtsh,dshm->dtm", weights, spread, precision=highest)
    start_state = state_prev.reshape(doc_count, inner, state_width).astype(jnp.float32)
    carried = jnp.einsum("dtn,dmn->dtm", query_proj, start_state, precision=highest)
    mixed_out = mixed_out + expand(jnp.exp(cum_decay)) * carried
    mixed_out = mixed_out + jnp.repeat(skip_weight, head_dim)[None, None, :] * chan_vals
    tail_weight = jnp.exp(cum_decay[:, -1:, :] - cum_decay) * step_size
    scaled_vals = expand(tail_weight) * chan_vals
    end_state = expand(jnp.exp(cum_decay[:, -1, :]))[:, :, None] * start_state
    end_state = end_state + jnp.einsum("dsm,dsn->dmn", scaled_vals, key_proj, precision=highest)
    new_conv = mixed_in[:, length - (kernel_len - 1) :].astype(jnp.bfloat16)
    gated = mixed_out * jax.nn.silu(gate_cols)
    gnormed = row_norm(gated, norm_scale).astype(jnp.bfloat16)
    partial_value = jnp.dot(
        gnormed.reshape(doc_count * length, inner), out_weight, preferred_element_type=jnp.float32
    )
    end_rounded = end_state.reshape(doc_count, head_count, head_dim * state_width).astype(
        jnp.bfloat16
    )
    return (partial_value, end_rounded, new_conv)


def shifted(value, axis, steps):
    count = lax.axis_size(axis)
    return lax.ppermute(value, axis, [(source, (source + steps) % count) for source in range(count)])


def gather_columns(value):
    count = lax.axis_size("mp")
    parts = [value] + [shifted(value, "mp", steps) for steps in range(1, count)]
    return jnp.concatenate(parts[::-1], axis=1)


def rotate_rows(value, block):
    count = lax.axis_size("mp")
    position = lax.axis_index("mp")
    doubled = jnp.concatenate([value, value], axis=0)
    return lax.dynamic_slice_in_dim(doubled, ((position + 1) % count) * block, count * block, 0)


def gather_from_behind(value):
    count = lax.axis_size("mp")
    sections = lax.axis_size("section")
    width = value.shape[1]
    position = lax.axis_index("mp")
    parts = []
    for steps in range(count):
        pairs = [
            (section * count + source, (section + 1) * count + (source + steps) % count)
            for section in range(sections - 1)
            for source in range(count)
        ]
        parts.append(lax.ppermute(value, ("section", "mp"), pairs))
    whole = jnp.concatenate(parts[::-1], axis=1)
    return whole, parts[0]


def scatter_sum(partial_value, base):
    count = lax.axis_size("mp")
    position = lax.axis_index("mp")
    rows = partial_value.shape[0]
    blocks = partial_value.astype(jnp.bfloat16).reshape(rows, count, -1)
    total = base + lax.dynamic_index_in_dim(blocks, position, 1, False).astype(jnp.float32)
    for steps in range(1, count):
        block = lax.dynamic_index_in_dim(blocks, (position + steps) % count, 1, False)
        total = total + shifted(block, "mp", steps).astype(jnp.float32)
    return total


def per_device(
    tokens,
    norm_gain,
    in_proj,
    conv_weight,
    conv_bias,
    step_bias,
    decay_rate,
    skip_gain,
    gate_gain,
    out_proj,
    kept_state,
    kept_conv,
    doc_owner,
    doc_slot,
    window_start,
):
    dp_count = lax.axis_size("dp")
    section_count = lax.axis_size("section")
    dp_idx = lax.axis_index("dp")
    section_idx = lax.axis_index("section")
    doc_count = window_start.shape[0]
    length = tokens.shape[0] // doc_count
    shard_width = tokens.shape[1]
    capacity = (doc_count + dp_count - 1) // dp_count
    owners = doc_owner.reshape(dp_count, doc_count)
    slots = doc_slot.reshape(dp_count, doc_count)
    positions = jnp.arange(doc_count)
    earlier = positions[:, None] > positions[None, :]
    same_owner = owners[:, :, None] == owners[:, None, :]
    owner_rank = jnp.sum(jnp.logical_and(same_owner, earlier[None]), axis=2)
    chosen = jnp.logical_and(
        (owners == dp_idx)[:, :, None],
        owner_rank[:, :, None] == jnp.arange(capacity)[None, None, :],
    )
    send_index = jnp.sum(jnp.where(chosen, slots[:, :, None], 0), axis=1).reshape(-1)
    heads_dev = kept_state.shape[2]
    state_cols = kept_state.shape[3]
    chans = conv_weight.shape[2]
    kernel_len = conv_weight.shape[1]
    send_state = kept_state[0][send_index].reshape(send_index.shape[0], -1)
    send_conv = kept_conv[0][send_index].reshape(send_index.shape[0], -1)
    state_size = send_state.shape[1]
    got_both = lax.all_to_all(
        jnp.concatenate([send_state, send_conv], axis=1), "dp", split_axis=0, concat_axis=0, tiled=True
    )
    my_owners = lax.dynamic_index_in_dim(owners, dp_idx, 0, keepdims=False)
    my_rank = lax.dynamic_index_in_dim(owner_rank, dp_idx, 0, keepdims=False)
    recv_row = my_owners * capacity + my_rank
    keep_flag = (window_start > 0).astype(jnp.float32)
    got_rows = got_both[recv_row].astype(jnp.float32) * keep_flag[:, None]
    state_start = got_rows[:, :state_size].reshape(doc_count, heads_dev, state_cols)
    conv_start = got_rows[:, state_size:].reshape(doc_count, kernel_len - 1, chans)
    gain_rotated = rotate_rows(norm_gain[0], shard_width)
    proj_rotated = rotate_rows(in_proj[0], shard_width)
    results = None
    incoming = None
    first_rows = None
    for phase in range(section_count):
        if incoming is None:
            current = tokens
            whole_rows = gather_columns(current)
            first_rows = whole_rows
        else:
            gathered, incoming = gather_from_behind(result)
            current = jnp.where(section_idx == 0, tokens, incoming)
            whole_rows = jnp.where(section_idx == 0, first_rows, gathered)
        normed = row_norm(whole_rows.astype(jnp.float32), gain_rotated).astype(jnp.bfloat16)
        projected = jnp.dot(normed, proj_rotated, preferred_element_type=jnp.float32)
        partial_value, state_new, conv_new = mix_channels(
            projected.reshape(doc_count, length, -1),
            conv_start,
            state_start,
            conv_weight[0],
            conv_bias[0],
            step_bias[0],
            decay_rate[0],
            skip_gain[0],
            gate_gain[0],
            out_proj[0],
        )
        result = scatter_sum(partial_value, current.astype(jnp.float32)).astype(jnp.bfloat16)
        results = (result, state_new, conv_new)
        incoming = result
    out_rows, new_states, new_convs = results
    return (out_rows[None], new_states[None], new_convs[None])


def solution(mesh):
    in_specs = (
        P("dp", "mp"),
        P("section", None),
        P("section", None, "mp"),
        P("section", None, "mp"),
        P("section", "mp"),
        P("section", "mp"),
        P("section", "mp"),
        P("section", "mp"),
        P("section", "mp"),
        P("section", "mp", None),
        P("section", "dp", "mp", None),
        P("section", "dp", None, "mp"),
        P(),
        P(),
        P("dp"),
    )
    out_specs = (
        P("section", "dp", "mp"),
        P("section", "dp", "mp", None),
        P("section", "dp", None, "mp"),
    )
    return jax.shard_map(
        per_device, mesh=mesh, in_specs=in_specs, out_specs=out_specs, check_vma=False
    )
```

```python
import jax
import jax.numpy as jnp
from jax import lax
from jax.sharding import PartitionSpec as P

epsilon = 1e-05
highest = lax.Precision.HIGHEST
three_pass = lax.Precision.HIGH


def from_behind(value, axis, steps):
    count = lax.axis_size(axis)
    first, last = (max(0, -steps), min(count, count - steps))
    return lax.ppermute(value, axis, [(source, source + steps) for source in range(first, last)])


def row_norm(values, norm_scale):
    inv_rms = lax.rsqrt(jnp.mean(values * values, axis=-1, keepdims=True) + epsilon)
    return values * inv_rms * norm_scale


def mix_channels(
    projected,
    conv_prev,
    state_prev,
    conv_kernel,
    conv_shift,
    step_shift,
    decay_speed,
    skip_weight,
    norm_scale,
    out_weight,
):
    doc_count = projected.shape[0]
    length = projected.shape[1]
    inner = norm_scale.shape[0]
    head_count = decay_speed.shape[0]
    head_dim = inner // head_count
    state_width = (projected.shape[2] - 2 * inner - head_count) // 2
    kernel_len = conv_kernel.shape[0]
    gate_cols = projected[:, :, :inner]
    mixed_in = projected[:, :, inner : 2 * inner + 2 * state_width]
    step_raw = projected[:, :, 2 * inner + 2 * state_width :]
    padded = jnp.concatenate([conv_prev, mixed_in], axis=1)
    conv_out = jnp.zeros_like(mixed_in) + conv_shift
    for offset in range(kernel_len):
        conv_out = conv_out + conv_kernel[offset] * padded[:, offset : offset + length]
    activated = jax.nn.silu(conv_out)
    chan_vals = activated[:, :, :inner]
    expander = (
        jnp.arange(inner)[None, :] // head_dim == jnp.arange(head_count)[:, None]
    ).astype(jnp.float32)

    def expand(per_head):
        return jnp.einsum("...h,hm->...m", per_head, expander, precision=highest)

    key_proj = activated[:, :, inner : inner + state_width]
    query_proj = activated[:, :, inner + state_width :]
    step_size = jax.nn.softplus(step_raw + step_shift)
    cum_decay = jnp.cumsum(-step_size * decay_speed, axis=1)
    pair_decay = cum_decay[:, :, None, :] - cum_decay[:, None, :, :]
    positions = jnp.arange(length)
    causal = positions[:, None] >= positions[None, :]
    decay = jnp.exp(jnp.where(causal[None, :, :, None], pair_decay, -1e30))
    scores = jnp.einsum("dtn,dsn->dts", query_proj, key_proj, precision=three_pass)
    weights = decay * scores[:, :, :, None] * step_size[:, None, :, :]
    spread = chan_vals[:, :, None, :] * expander[None, None, :, :]
    mixed_out = jnp.einsum("dtsh,dshm->dtm", weights, spread, precision=three_pass)
    start_state = state_prev.reshape(doc_count, inner, state_width).astype(jnp.float32)
    carried = jnp.einsum("dtn,dmn->dtm", query_proj, start_state, precision=three_pass)
    mixed_out = mixed_out + expand(jnp.exp(cum_decay)) * carried
    mixed_out = mixed_out + jnp.repeat(skip_weight, head_dim)[None, None, :] * chan_vals
    tail_weight = jnp.exp(cum_decay[:, -1:, :] - cum_decay) * step_size
    scaled_vals = expand(tail_weight) * chan_vals
    end_state = expand(jnp.exp(cum_decay[:, -1, :]))[:, :, None] * start_state
    end_state = end_state + jnp.einsum("dsm,dsn->dmn", scaled_vals, key_proj, precision=three_pass)
    new_conv = mixed_in[:, length - (kernel_len - 1) :].astype(jnp.bfloat16)
    gated = mixed_out * jax.nn.silu(gate_cols)
    gnormed = row_norm(gated, norm_scale).astype(jnp.bfloat16)
    partial_value = jnp.dot(
        gnormed.reshape(doc_count * length, inner), out_weight, preferred_element_type=jnp.float32
    )
    end_rounded = end_state.reshape(doc_count, head_count, head_dim * state_width).astype(
        jnp.bfloat16
    )
    return (partial_value, end_rounded, new_conv)


def shifted(value, axis, steps):
    count = lax.axis_size(axis)
    return lax.ppermute(value, axis, [(source, (source + steps) % count) for source in range(count)])


def gather_columns(value):
    count = lax.axis_size("mp")
    parts = [value] + [shifted(value, "mp", steps) for steps in range(1, count)]
    return jnp.concatenate(parts[::-1], axis=1)


def rotate_rows(value, block):
    count = lax.axis_size("mp")
    position = lax.axis_index("mp")
    doubled = jnp.concatenate([value, value], axis=0)
    return lax.dynamic_slice_in_dim(doubled, ((position + 1) % count) * block, count * block, 0)


def gather_from_behind(value):
    count = lax.axis_size("mp")
    sections = lax.axis_size("section")
    width = value.shape[1]
    position = lax.axis_index("mp")
    parts = []
    for steps in range(count):
        pairs = [
            (section * count + source, (section + 1) * count + (source + steps) % count)
            for section in range(sections - 1)
            for source in range(count)
        ]
        parts.append(lax.ppermute(value, ("section", "mp"), pairs))
    whole = jnp.concatenate(parts[::-1], axis=1)
    return whole, parts[0]


def scatter_sum(partial_value, base):
    count = lax.axis_size("mp")
    position = lax.axis_index("mp")
    rows = partial_value.shape[0]
    blocks = partial_value.astype(jnp.bfloat16).reshape(rows, count, -1)
    total = base + lax.dynamic_index_in_dim(blocks, position, 1, False).astype(jnp.float32)
    for steps in range(1, count):
        block = lax.dynamic_index_in_dim(blocks, (position + steps) % count, 1, False)
        total = total + shifted(block, "mp", steps).astype(jnp.float32)
    return total


def per_device(
    tokens,
    norm_gain,
    in_proj,
    conv_weight,
    conv_bias,
    step_bias,
    decay_rate,
    skip_gain,
    gate_gain,
    out_proj,
    kept_state,
    kept_conv,
    doc_owner,
    doc_slot,
    window_start,
):
    dp_count = lax.axis_size("dp")
    section_count = lax.axis_size("section")
    dp_idx = lax.axis_index("dp")
    section_idx = lax.axis_index("section")
    doc_count = window_start.shape[0]
    length = tokens.shape[0] // doc_count
    shard_width = tokens.shape[1]
    capacity = (doc_count + dp_count - 1) // dp_count
    owners = doc_owner.reshape(dp_count, doc_count)
    slots = doc_slot.reshape(dp_count, doc_count)
    positions = jnp.arange(doc_count)
    earlier = positions[:, None] > positions[None, :]
    same_owner = owners[:, :, None] == owners[:, None, :]
    owner_rank = jnp.sum(jnp.logical_and(same_owner, earlier[None]), axis=2)
    chosen = jnp.logical_and(
        (owners == dp_idx)[:, :, None],
        owner_rank[:, :, None] == jnp.arange(capacity)[None, None, :],
    )
    send_index = jnp.sum(jnp.where(chosen, slots[:, :, None], 0), axis=1).reshape(-1)
    heads_dev = kept_state.shape[2]
    state_cols = kept_state.shape[3]
    chans = conv_weight.shape[2]
    kernel_len = conv_weight.shape[1]
    send_state = kept_state[0][send_index].reshape(send_index.shape[0], -1)
    send_conv = kept_conv[0][send_index].reshape(send_index.shape[0], -1)
    state_size = send_state.shape[1]
    got_both = lax.all_to_all(
        jnp.concatenate([send_state, send_conv], axis=1), "dp", split_axis=0, concat_axis=0, tiled=True
    )
    my_owners = lax.dynamic_index_in_dim(owners, dp_idx, 0, keepdims=False)
    my_rank = lax.dynamic_index_in_dim(owner_rank, dp_idx, 0, keepdims=False)
    recv_row = my_owners * capacity + my_rank
    keep_flag = (window_start > 0).astype(jnp.float32)
    got_rows = got_both[recv_row].astype(jnp.float32) * keep_flag[:, None]
    state_start = got_rows[:, :state_size].reshape(doc_count, heads_dev, state_cols)
    conv_start = got_rows[:, state_size:].reshape(doc_count, kernel_len - 1, chans)
    gain_rotated = rotate_rows(norm_gain[0], shard_width)
    proj_rotated = rotate_rows(in_proj[0], shard_width)
    results = None
    incoming = None
    first_rows = None
    for phase in range(section_count):
        if incoming is None:
            current = tokens
            whole_rows = gather_columns(current)
            first_rows = whole_rows
        else:
            gathered, incoming = gather_from_behind(result)
            current = jnp.where(section_idx == 0, tokens, incoming)
            whole_rows = jnp.where(section_idx == 0, first_rows, gathered)
        normed = row_norm(whole_rows.astype(jnp.float32), gain_rotated).astype(jnp.bfloat16)
        projected = jnp.dot(normed, proj_rotated, preferred_element_type=jnp.float32)
        partial_value, state_new, conv_new = mix_channels(
            projected.reshape(doc_count, length, -1),
            conv_start,
            state_start,
            conv_weight[0],
            conv_bias[0],
            step_bias[0],
            decay_rate[0],
            skip_gain[0],
            gate_gain[0],
            out_proj[0],
        )
        result = scatter_sum(partial_value, current.astype(jnp.float32)).astype(jnp.bfloat16)
        results = (result, state_new, conv_new)
        incoming = result
    out_rows, new_states, new_convs = results
    return (out_rows[None], new_states[None], new_convs[None])


def solution(mesh):
    in_specs = (
        P("dp", "mp"),
        P("section", None),
        P("section", None, "mp"),
        P("section", None, "mp"),
        P("section", "mp"),
        P("section", "mp"),
        P("section", "mp"),
        P("section", "mp"),
        P("section", "mp"),
        P("section", "mp", None),
        P("section", "dp", "mp", None),
        P("section", "dp", None, "mp"),
        P(),
        P(),
        P("dp"),
    )
    out_specs = (
        P("section", "dp", "mp"),
        P("section", "dp", "mp", None),
        P("section", "dp", None, "mp"),
    )
    return jax.shard_map(
        per_device, mesh=mesh, in_specs=in_specs, out_specs=out_specs, check_vma=False
    )
```

```python
import jax
import jax.numpy as jnp
from jax import lax
from jax.sharding import PartitionSpec as P

epsilon = 1e-05
highest = lax.Precision.HIGHEST
three_pass = lax.Precision.HIGH


def from_behind(value, axis, steps):
    count = lax.axis_size(axis)
    first, last = (max(0, -steps), min(count, count - steps))
    return lax.ppermute(value, axis, [(source, source + steps) for source in range(first, last)])


def row_norm(values, norm_scale):
    inv_rms = lax.rsqrt(jnp.mean(values * values, axis=-1, keepdims=True) + epsilon)
    return values * inv_rms * norm_scale


def mix_channels(
    projected,
    conv_prev,
    state_prev,
    conv_kernel,
    conv_shift,
    step_shift,
    decay_speed,
    skip_weight,
    norm_scale,
    out_weight,
):
    doc_count = projected.shape[0]
    length = projected.shape[1]
    inner = norm_scale.shape[0]
    head_count = decay_speed.shape[0]
    head_dim = inner // head_count
    state_width = (projected.shape[2] - 2 * inner - head_count) // 2
    kernel_len = conv_kernel.shape[0]
    gate_cols = projected[:, :, :inner]
    mixed_in = projected[:, :, inner : 2 * inner + 2 * state_width]
    step_raw = projected[:, :, 2 * inner + 2 * state_width :]
    padded = jnp.concatenate([conv_prev, mixed_in], axis=1)
    conv_out = jnp.zeros_like(mixed_in) + conv_shift
    for offset in range(kernel_len):
        conv_out = conv_out + conv_kernel[offset] * padded[:, offset : offset + length]
    activated = jax.nn.silu(conv_out)
    chan_vals = activated[:, :, :inner]
    expander = (
        jnp.arange(inner)[None, :] // head_dim == jnp.arange(head_count)[:, None]
    ).astype(jnp.float32)

    def expand(per_head):
        return jnp.einsum("...h,hm->...m", per_head, expander, precision=highest)

    key_proj = activated[:, :, inner : inner + state_width]
    query_proj = activated[:, :, inner + state_width :]
    step_size = jax.nn.softplus(step_raw + step_shift)
    cum_decay = jnp.cumsum(-step_size * decay_speed, axis=1)
    pair_decay = cum_decay[:, :, None, :] - cum_decay[:, None, :, :]
    positions = jnp.arange(length)
    causal = positions[:, None] >= positions[None, :]
    decay = jnp.exp(jnp.where(causal[None, :, :, None], pair_decay, -1e30))
    scores = jnp.einsum("dtn,dsn->dts", query_proj, key_proj, precision=three_pass)
    weights = decay * scores[:, :, :, None] * step_size[:, None, :, :]
    spread = chan_vals[:, :, None, :] * expander[None, None, :, :]
    mixed_out = jnp.einsum("dtsh,dshm->dtm", weights, spread, precision=three_pass)
    start_state = state_prev.reshape(doc_count, inner, state_width).astype(jnp.float32)
    carried = jnp.einsum("dtn,dmn->dtm", query_proj, start_state, precision=three_pass)
    mixed_out = mixed_out + expand(jnp.exp(cum_decay)) * carried
    mixed_out = mixed_out + jnp.repeat(skip_weight, head_dim)[None, None, :] * chan_vals
    tail_weight = jnp.exp(cum_decay[:, -1:, :] - cum_decay) * step_size
    scaled_vals = expand(tail_weight) * chan_vals
    end_state = expand(jnp.exp(cum_decay[:, -1, :]))[:, :, None] * start_state
    end_state = end_state + jnp.einsum("dsm,dsn->dmn", scaled_vals, key_proj, precision=three_pass)
    new_conv = mixed_in[:, length - (kernel_len - 1) :].astype(jnp.bfloat16)
    gated = mixed_out * jax.nn.silu(gate_cols)
    gnormed = row_norm(gated, norm_scale).astype(jnp.bfloat16)
    partial_value = jnp.dot(
        gnormed.reshape(doc_count * length, inner), out_weight, preferred_element_type=jnp.float32
    )
    end_rounded = end_state.reshape(doc_count, head_count, head_dim * state_width).astype(
        jnp.bfloat16
    )
    return (partial_value, end_rounded, new_conv)


def shifted(value, axis, steps):
    count = lax.axis_size(axis)
    return lax.ppermute(value, axis, [(source, (source + steps) % count) for source in range(count)])


def gather_columns(value):
    count = lax.axis_size("mp")
    parts = [value] + [shifted(value, "mp", steps) for steps in range(1, count)]
    return jnp.concatenate(parts[::-1], axis=1)


def rotate_rows(value, block):
    count = lax.axis_size("mp")
    position = lax.axis_index("mp")
    doubled = jnp.concatenate([value, value], axis=0)
    return lax.dynamic_slice_in_dim(doubled, ((position + 1) % count) * block, count * block, 0)


def gather_from_behind(value):
    count = lax.axis_size("mp")
    sections = lax.axis_size("section")
    width = value.shape[1]
    position = lax.axis_index("mp")
    parts = []
    for steps in range(count):
        pairs = [
            (section * count + source, (section + 1) * count + (source + steps) % count)
            for section in range(sections - 1)
            for source in range(count)
        ]
        parts.append(lax.ppermute(value, ("section", "mp"), pairs))
    whole = jnp.concatenate(parts[::-1], axis=1)
    return whole, parts[0]


def scatter_sum(partial_value, base):
    count = lax.axis_size("mp")
    position = lax.axis_index("mp")
    rows = partial_value.shape[0]
    blocks = partial_value.astype(jnp.bfloat16).reshape(rows, count, -1)
    total = base + lax.dynamic_index_in_dim(blocks, position, 1, False).astype(jnp.float32)
    for steps in range(1, count):
        block = lax.dynamic_index_in_dim(blocks, (position + steps) % count, 1, False)
        total = total + shifted(block, "mp", steps).astype(jnp.float32)
    return total


def per_device(
    tokens,
    norm_gain,
    in_proj,
    conv_weight,
    conv_bias,
    step_bias,
    decay_rate,
    skip_gain,
    gate_gain,
    out_proj,
    kept_state,
    kept_conv,
    doc_owner,
    doc_slot,
    window_start,
):
    dp_count = lax.axis_size("dp")
    section_count = lax.axis_size("section")
    dp_idx = lax.axis_index("dp")
    section_idx = lax.axis_index("section")
    doc_count = window_start.shape[0]
    length = tokens.shape[0] // doc_count
    shard_width = tokens.shape[1]
    capacity = (doc_count + dp_count - 1) // dp_count
    owners = doc_owner.reshape(dp_count, doc_count)
    slots = doc_slot.reshape(dp_count, doc_count)
    positions = jnp.arange(doc_count)
    earlier = positions[:, None] > positions[None, :]
    same_owner = owners[:, :, None] == owners[:, None, :]
    owner_rank = jnp.sum(jnp.logical_and(same_owner, earlier[None]), axis=2)
    chosen = jnp.logical_and(
        (owners == dp_idx)[:, :, None],
        owner_rank[:, :, None] == jnp.arange(capacity)[None, None, :],
    )
    send_index = jnp.sum(jnp.where(chosen, slots[:, :, None], 0), axis=1).reshape(-1)
    heads_dev = kept_state.shape[2]
    state_cols = kept_state.shape[3]
    chans = conv_weight.shape[2]
    kernel_len = conv_weight.shape[1]
    send_state = kept_state[0][send_index]
    send_conv = kept_conv[0][send_index]
    got_conv = lax.all_to_all(send_conv, "dp", split_axis=0, concat_axis=0, tiled=True)
    got_state = lax.all_to_all(send_state, "dp", split_axis=0, concat_axis=0, tiled=True)
    my_owners = lax.dynamic_index_in_dim(owners, dp_idx, 0, keepdims=False)
    my_rank = lax.dynamic_index_in_dim(owner_rank, dp_idx, 0, keepdims=False)
    recv_row = my_owners * capacity + my_rank
    keep_flag = (window_start > 0).astype(jnp.float32)
    state_start = got_state[recv_row] * keep_flag.astype(jnp.bfloat16)[:, None, None]
    conv_start = got_conv[recv_row].astype(jnp.float32) * keep_flag[:, None, None]
    gain_rotated = rotate_rows(norm_gain[0], shard_width)
    proj_rotated = rotate_rows(in_proj[0], shard_width)
    results = None
    incoming = None
    first_rows = None
    for phase in range(section_count):
        if incoming is None:
            current = tokens
            whole_rows = gather_columns(current)
            first_rows = whole_rows
        else:
            gathered, incoming = gather_from_behind(result)
            current = jnp.where(section_idx == 0, tokens, incoming)
            whole_rows = jnp.where(section_idx == 0, first_rows, gathered)
        normed = row_norm(whole_rows.astype(jnp.float32), gain_rotated).astype(jnp.bfloat16)
        projected = jnp.dot(normed, proj_rotated, preferred_element_type=jnp.float32)
        partial_value, state_new, conv_new = mix_channels(
            projected.reshape(doc_count, length, -1),
            conv_start,
            state_start,
            conv_weight[0],
            conv_bias[0],
            step_bias[0],
            decay_rate[0],
            skip_gain[0],
            gate_gain[0],
            out_proj[0],
        )
        result = scatter_sum(partial_value, current.astype(jnp.float32)).astype(jnp.bfloat16)
        results = (result, state_new, conv_new)
        incoming = result
    out_rows, new_states, new_convs = results
    return (out_rows[None], new_states[None], new_convs[None])


def solution(mesh):
    in_specs = (
        P("dp", "mp"),
        P("section", None),
        P("section", None, "mp"),
        P("section", None, "mp"),
        P("section", "mp"),
        P("section", "mp"),
        P("section", "mp"),
        P("section", "mp"),
        P("section", "mp"),
        P("section", "mp", None),
        P("section", "dp", "mp", None),
        P("section", "dp", None, "mp"),
        P(),
        P(),
        P("dp"),
    )
    out_specs = (
        P("section", "dp", "mp"),
        P("section", "dp", "mp", None),
        P("section", "dp", None, "mp"),
    )
    return jax.shard_map(
        per_device, mesh=mesh, in_specs=in_specs, out_specs=out_specs, check_vma=False
    )
```

```python
import jax
import jax.numpy as jnp
from jax import lax
from jax.sharding import PartitionSpec as P

epsilon = 1e-05
highest = lax.Precision.HIGHEST
three_pass = lax.Precision.HIGH


def from_behind(value, axis, steps):
    count = lax.axis_size(axis)
    first, last = (max(0, -steps), min(count, count - steps))
    return lax.ppermute(value, axis, [(source, source + steps) for source in range(first, last)])


def row_norm(values, norm_scale):
    inv_rms = lax.rsqrt(jnp.mean(values * values, axis=-1, keepdims=True) + epsilon)
    return values * inv_rms * norm_scale


def mix_channels(
    projected,
    conv_prev,
    state_prev,
    conv_kernel,
    conv_shift,
    step_shift,
    decay_speed,
    skip_weight,
    norm_scale,
    out_weight,
):
    doc_count = projected.shape[0]
    length = projected.shape[1]
    inner = norm_scale.shape[0]
    head_count = decay_speed.shape[0]
    head_dim = inner // head_count
    state_width = (projected.shape[2] - 2 * inner - head_count) // 2
    kernel_len = conv_kernel.shape[0]
    gate_cols = projected[:, :, :inner]
    mixed_in = projected[:, :, inner : 2 * inner + 2 * state_width]
    step_raw = projected[:, :, 2 * inner + 2 * state_width :]
    padded = jnp.concatenate([conv_prev, mixed_in], axis=1)
    conv_out = jnp.zeros_like(mixed_in) + conv_shift
    for offset in range(kernel_len):
        conv_out = conv_out + conv_kernel[offset] * padded[:, offset : offset + length]
    activated = jax.nn.silu(conv_out)
    chan_vals = activated[:, :, :inner]
    expander = (
        jnp.arange(inner)[None, :] // head_dim == jnp.arange(head_count)[:, None]
    ).astype(jnp.float32)

    def expand(per_head):
        return jnp.einsum("...h,hm->...m", per_head, expander, precision=highest)

    key_proj = activated[:, :, inner : inner + state_width]
    query_proj = activated[:, :, inner + state_width :]
    step_size = jax.nn.softplus(step_raw + step_shift)
    cum_decay = jnp.cumsum(-step_size * decay_speed, axis=1)
    pair_decay = cum_decay[:, :, None, :] - cum_decay[:, None, :, :]
    positions = jnp.arange(length)
    causal = positions[:, None] >= positions[None, :]
    decay = jnp.exp(jnp.where(causal[None, :, :, None], pair_decay, -1e30))
    scores = jnp.einsum("dtn,dsn->dts", query_proj, key_proj, precision=three_pass)
    weights = decay * scores[:, :, :, None] * step_size[:, None, :, :]
    spread = chan_vals[:, :, None, :] * expander[None, None, :, :]
    mixed_out = jnp.einsum("dtsh,dshm->dtm", weights, spread, precision=three_pass)
    start_state = state_prev.reshape(doc_count, inner, state_width).astype(jnp.float32)
    carried = jnp.einsum("dtn,dmn->dtm", query_proj, start_state, precision=three_pass)
    mixed_out = mixed_out + expand(jnp.exp(cum_decay)) * carried
    mixed_out = mixed_out + jnp.repeat(skip_weight, head_dim)[None, None, :] * chan_vals
    tail_weight = jnp.exp(cum_decay[:, -1:, :] - cum_decay) * step_size
    scaled_vals = expand(tail_weight) * chan_vals
    end_state = expand(jnp.exp(cum_decay[:, -1, :]))[:, :, None] * start_state
    end_state = end_state + jnp.einsum("dsm,dsn->dmn", scaled_vals, key_proj, precision=three_pass)
    new_conv = mixed_in[:, length - (kernel_len - 1) :].astype(jnp.bfloat16)
    gated = mixed_out * jax.nn.silu(gate_cols)
    gnormed = row_norm(gated, norm_scale).astype(jnp.bfloat16)
    partial_value = gnormed.reshape(doc_count * length, inner)
    end_rounded = end_state.reshape(doc_count, head_count, head_dim * state_width).astype(
        jnp.bfloat16
    )
    return (partial_value, end_rounded, new_conv)


def shifted(value, axis, steps):
    count = lax.axis_size(axis)
    return lax.ppermute(value, axis, [(source, (source + steps) % count) for source in range(count)])


def gather_columns(value):
    count = lax.axis_size("mp")
    parts = [value] + [shifted(value, "mp", steps) for steps in range(1, count)]
    return jnp.concatenate(parts[::-1], axis=1)


def rotate_rows(value, block):
    count = lax.axis_size("mp")
    position = lax.axis_index("mp")
    doubled = jnp.concatenate([value, value], axis=0)
    return lax.dynamic_slice_in_dim(doubled, ((position + 1) % count) * block, count * block, 0)


def gather_from_behind(value):
    count = lax.axis_size("mp")
    sections = lax.axis_size("section")
    width = value.shape[1]
    position = lax.axis_index("mp")
    parts = []
    for steps in range(count):
        pairs = [
            (section * count + source, (section + 1) * count + (source + steps) % count)
            for section in range(sections - 1)
            for source in range(count)
        ]
        parts.append(lax.ppermute(value, ("section", "mp"), pairs))
    whole = jnp.concatenate(parts[::-1], axis=1)
    return whole, parts[0]


def column_blocks(out_weight):
    count = lax.axis_size("mp")
    position = lax.axis_index("mp")
    width = out_weight.shape[1] // count
    return [
        lax.dynamic_slice_in_dim(out_weight, ((position + steps) % count) * width, width, 1)
        for steps in range(count)
    ]


def scatter_sum(gnormed, weight_blocks, base):
    total = base
    for steps, weight_block in enumerate(weight_blocks):
        block = jnp.dot(gnormed, weight_block, preferred_element_type=jnp.float32).astype(jnp.bfloat16)
        if steps > 0:
            block = shifted(block, "mp", steps)
        total = total + block.astype(jnp.float32)
    return total


def per_device(
    tokens,
    norm_gain,
    in_proj,
    conv_weight,
    conv_bias,
    step_bias,
    decay_rate,
    skip_gain,
    gate_gain,
    out_proj,
    kept_state,
    kept_conv,
    doc_owner,
    doc_slot,
    window_start,
):
    dp_count = lax.axis_size("dp")
    section_count = lax.axis_size("section")
    dp_idx = lax.axis_index("dp")
    section_idx = lax.axis_index("section")
    doc_count = window_start.shape[0]
    length = tokens.shape[0] // doc_count
    shard_width = tokens.shape[1]
    capacity = (doc_count + dp_count - 1) // dp_count
    owners = doc_owner.reshape(dp_count, doc_count)
    slots = doc_slot.reshape(dp_count, doc_count)
    positions = jnp.arange(doc_count)
    earlier = positions[:, None] > positions[None, :]
    same_owner = owners[:, :, None] == owners[:, None, :]
    owner_rank = jnp.sum(jnp.logical_and(same_owner, earlier[None]), axis=2)
    chosen = jnp.logical_and(
        (owners == dp_idx)[:, :, None],
        owner_rank[:, :, None] == jnp.arange(capacity)[None, None, :],
    )
    send_index = jnp.sum(jnp.where(chosen, slots[:, :, None], 0), axis=1).reshape(-1)
    heads_dev = kept_state.shape[2]
    state_cols = kept_state.shape[3]
    chans = conv_weight.shape[2]
    kernel_len = conv_weight.shape[1]
    send_state = kept_state[0][send_index]
    send_conv = kept_conv[0][send_index]
    got_conv = lax.all_to_all(send_conv, "dp", split_axis=0, concat_axis=0, tiled=True)
    got_state = lax.all_to_all(send_state, "dp", split_axis=0, concat_axis=0, tiled=True)
    my_owners = lax.dynamic_index_in_dim(owners, dp_idx, 0, keepdims=False)
    my_rank = lax.dynamic_index_in_dim(owner_rank, dp_idx, 0, keepdims=False)
    recv_row = my_owners * capacity + my_rank
    keep_flag = (window_start > 0).astype(jnp.float32)
    state_start = got_state[recv_row] * keep_flag.astype(jnp.bfloat16)[:, None, None]
    conv_start = got_conv[recv_row].astype(jnp.float32) * keep_flag[:, None, None]
    gain_rotated = rotate_rows(norm_gain[0], shard_width)
    proj_rotated = rotate_rows(in_proj[0], shard_width)
    weight_blocks = column_blocks(out_proj[0])
    results = None
    incoming = None
    first_rows = None
    for phase in range(section_count):
        if incoming is None:
            current = tokens
            whole_rows = gather_columns(current)
            first_rows = whole_rows
        else:
            gathered, incoming = gather_from_behind(result)
            current = jnp.where(section_idx == 0, tokens, incoming)
            whole_rows = jnp.where(section_idx == 0, first_rows, gathered)
        normed = row_norm(whole_rows.astype(jnp.float32), gain_rotated).astype(jnp.bfloat16)
        projected = jnp.dot(normed, proj_rotated, preferred_element_type=jnp.float32)
        partial_value, state_new, conv_new = mix_channels(
            projected.reshape(doc_count, length, -1),
            conv_start,
            state_start,
            conv_weight[0],
            conv_bias[0],
            step_bias[0],
            decay_rate[0],
            skip_gain[0],
            gate_gain[0],
            out_proj[0],
        )
        result = scatter_sum(partial_value, weight_blocks, current.astype(jnp.float32)).astype(jnp.bfloat16)
        results = (result, state_new, conv_new)
        incoming = result
    out_rows, new_states, new_convs = results
    return (out_rows[None], new_states[None], new_convs[None])


def solution(mesh):
    in_specs = (
        P("dp", "mp"),
        P("section", None),
        P("section", None, "mp"),
        P("section", None, "mp"),
        P("section", "mp"),
        P("section", "mp"),
        P("section", "mp"),
        P("section", "mp"),
        P("section", "mp"),
        P("section", "mp", None),
        P("section", "dp", "mp", None),
        P("section", "dp", None, "mp"),
        P(),
        P(),
        P("dp"),
    )
    out_specs = (
        P("section", "dp", "mp"),
        P("section", "dp", "mp", None),
        P("section", "dp", None, "mp"),
    )
    return jax.shard_map(
        per_device, mesh=mesh, in_specs=in_specs, out_specs=out_specs, check_vma=False
    )
```

```python
import jax
import jax.numpy as jnp
from jax import lax
from jax.sharding import PartitionSpec as P

epsilon = 1e-05
highest = lax.Precision.HIGHEST
three_pass = lax.Precision.HIGH


def from_behind(value, axis, steps):
    count = lax.axis_size(axis)
    first, last = (max(0, -steps), min(count, count - steps))
    return lax.ppermute(value, axis, [(source, source + steps) for source in range(first, last)])


def row_norm(values, norm_scale):
    inv_rms = lax.rsqrt(jnp.mean(values * values, axis=-1, keepdims=True) + epsilon)
    return values * inv_rms * norm_scale


def mix_channels(
    projected,
    conv_prev,
    state_prev,
    conv_kernel,
    conv_shift,
    step_shift,
    decay_speed,
    skip_weight,
    norm_scale,
    out_weight,
):
    doc_count = projected.shape[0]
    length = projected.shape[1]
    inner = norm_scale.shape[0]
    head_count = decay_speed.shape[0]
    head_dim = inner // head_count
    state_width = (projected.shape[2] - 2 * inner - head_count) // 2
    kernel_len = conv_kernel.shape[0]
    gate_cols = projected[:, :, :inner]
    mixed_in = projected[:, :, inner : 2 * inner + 2 * state_width]
    step_raw = projected[:, :, 2 * inner + 2 * state_width :]
    padded = jnp.concatenate([conv_prev, mixed_in], axis=1)
    conv_out = jnp.zeros_like(mixed_in) + conv_shift
    for offset in range(kernel_len):
        conv_out = conv_out + conv_kernel[offset] * padded[:, offset : offset + length]
    activated = jax.nn.silu(conv_out)
    chan_vals = activated[:, :, :inner]
    expander = (
        jnp.arange(inner)[None, :] // head_dim == jnp.arange(head_count)[:, None]
    ).astype(jnp.float32)

    def expand(per_head):
        return jnp.einsum("...h,hm->...m", per_head, expander, precision=highest)

    key_proj = activated[:, :, inner : inner + state_width]
    query_proj = activated[:, :, inner + state_width :]
    step_size = jax.nn.softplus(step_raw + step_shift)
    cum_decay = jnp.cumsum(-step_size * decay_speed, axis=1)
    pair_decay = cum_decay[:, :, None, :] - cum_decay[:, None, :, :]
    positions = jnp.arange(length)
    causal = positions[:, None] >= positions[None, :]
    decay = jnp.exp(jnp.where(causal[None, :, :, None], pair_decay, -1e30))
    scores = jnp.einsum("dtn,dsn->dts", query_proj, key_proj, precision=three_pass)
    weights = decay * scores[:, :, :, None] * step_size[:, None, :, :]
    spread = chan_vals[:, :, None, :] * expander[None, None, :, :]
    mixed_out = jnp.einsum("dtsh,dshm->dtm", weights, spread, precision=three_pass)
    start_state = state_prev.reshape(doc_count, inner, state_width).astype(jnp.float32)
    carried = jnp.einsum("dtn,dmn->dtm", query_proj, start_state, precision=three_pass)
    mixed_out = mixed_out + expand(jnp.exp(cum_decay)) * carried
    mixed_out = mixed_out + jnp.repeat(skip_weight, head_dim)[None, None, :] * chan_vals
    tail_weight = jnp.exp(cum_decay[:, -1:, :] - cum_decay) * step_size
    scaled_vals = expand(tail_weight) * chan_vals
    end_state = expand(jnp.exp(cum_decay[:, -1, :]))[:, :, None] * start_state
    end_state = end_state + jnp.einsum("dsm,dsn->dmn", scaled_vals, key_proj, precision=three_pass)
    new_conv = mixed_in[:, length - (kernel_len - 1) :].astype(jnp.bfloat16)
    gated = mixed_out * jax.nn.silu(gate_cols)
    gnormed = row_norm(gated, norm_scale).astype(jnp.bfloat16)
    partial_value = gnormed.reshape(doc_count * length, inner)
    end_rounded = end_state.reshape(doc_count, head_count, head_dim * state_width).astype(
        jnp.bfloat16
    )
    return (partial_value, end_rounded, new_conv)


def shifted(value, axis, steps):
    count = lax.axis_size(axis)
    return lax.ppermute(value, axis, [(source, (source + steps) % count) for source in range(count)])


def gather_columns(value):
    count = lax.axis_size("mp")
    parts = [value] + [shifted(value, "mp", steps) for steps in range(1, count)]
    return jnp.concatenate(parts[::-1], axis=1)


def rotate_rows(value, block):
    count = lax.axis_size("mp")
    position = lax.axis_index("mp")
    doubled = jnp.concatenate([value, value], axis=0)
    return lax.dynamic_slice_in_dim(doubled, ((position + 1) % count) * block, count * block, 0)


def gather_from_behind(value):
    count = lax.axis_size("mp")
    sections = lax.axis_size("section")
    width = value.shape[1]
    position = lax.axis_index("mp")
    parts = []
    for steps in range(count):
        pairs = [
            (section * count + source, (section + 1) * count + (source + steps) % count)
            for section in range(sections - 1)
            for source in range(count)
        ]
        parts.append(lax.ppermute(value, ("section", "mp"), pairs))
    whole = jnp.concatenate(parts[::-1], axis=1)
    return whole, parts[0]


def column_blocks(out_weight):
    count = lax.axis_size("mp")
    position = lax.axis_index("mp")
    width = out_weight.shape[1] // count
    return [
        lax.dynamic_slice_in_dim(out_weight, ((position + steps) % count) * width, width, 1)
        for steps in range(count)
    ]


def scatter_sum(gnormed, weight_blocks, base):
    total = base
    for steps, weight_block in enumerate(weight_blocks):
        block = jnp.dot(gnormed, weight_block, preferred_element_type=jnp.float32).astype(jnp.bfloat16)
        if steps > 0:
            block = shifted(block, "mp", steps)
        total = total + block.astype(jnp.float32)
    return total


def per_device(
    tokens,
    norm_gain,
    in_proj,
    conv_weight,
    conv_bias,
    step_bias,
    decay_rate,
    skip_gain,
    gate_gain,
    out_proj,
    kept_state,
    kept_conv,
    doc_owner,
    doc_slot,
    window_start,
):
    dp_count = lax.axis_size("dp")
    section_count = lax.axis_size("section")
    dp_idx = lax.axis_index("dp")
    section_idx = lax.axis_index("section")
    doc_count = window_start.shape[0]
    length = tokens.shape[0] // doc_count
    shard_width = tokens.shape[1]
    capacity = (doc_count + dp_count - 1) // dp_count
    owners = doc_owner.reshape(dp_count, doc_count)
    slots = doc_slot.reshape(dp_count, doc_count)
    positions = jnp.arange(doc_count)
    earlier = positions[:, None] > positions[None, :]
    same_owner = owners[:, :, None] == owners[:, None, :]
    owner_rank = jnp.sum(jnp.logical_and(same_owner, earlier[None]), axis=2)
    chosen = jnp.logical_and(
        (owners == dp_idx)[:, :, None],
        owner_rank[:, :, None] == jnp.arange(capacity)[None, None, :],
    )
    send_index = jnp.sum(jnp.where(chosen, slots[:, :, None], 0), axis=1).reshape(-1)
    heads_dev = kept_state.shape[2]
    state_cols = kept_state.shape[3]
    chans = conv_weight.shape[2]
    kernel_len = conv_weight.shape[1]
    slot_count = kept_state.shape[1]
    send_pick = (send_index[:, None] == jnp.arange(slot_count)[None, :]).astype(jnp.bfloat16)

    def select_rows(picker, rows):
        picked = jnp.dot(picker, rows.reshape(rows.shape[0], -1), preferred_element_type=jnp.float32)
        return picked.astype(jnp.bfloat16).reshape((picker.shape[0],) + rows.shape[1:])

    send_state = select_rows(send_pick, kept_state[0])
    send_conv = select_rows(send_pick, kept_conv[0])
    got_conv = lax.all_to_all(send_conv, "dp", split_axis=0, concat_axis=0, tiled=True)
    got_state = lax.all_to_all(send_state, "dp", split_axis=0, concat_axis=0, tiled=True)
    my_owners = lax.dynamic_index_in_dim(owners, dp_idx, 0, keepdims=False)
    my_rank = lax.dynamic_index_in_dim(owner_rank, dp_idx, 0, keepdims=False)
    recv_row = my_owners * capacity + my_rank
    keep_flag = (window_start > 0).astype(jnp.float32)
    recv_pick = (recv_row[:, None] == jnp.arange(got_state.shape[0])[None, :]).astype(jnp.float32)
    recv_pick = (recv_pick * keep_flag[:, None]).astype(jnp.bfloat16)
    state_start = select_rows(recv_pick, got_state)
    conv_start = select_rows(recv_pick, got_conv).astype(jnp.float32)
    gain_rotated = rotate_rows(norm_gain[0], shard_width)
    proj_rotated = rotate_rows(in_proj[0], shard_width)
    weight_blocks = column_blocks(out_proj[0])
    results = None
    incoming = None
    first_rows = None
    for phase in range(section_count):
        if incoming is None:
            current = tokens
            whole_rows = gather_columns(current)
            first_rows = whole_rows
        else:
            gathered, incoming = gather_from_behind(result)
            current = jnp.where(section_idx == 0, tokens, incoming)
            whole_rows = jnp.where(section_idx == 0, first_rows, gathered)
        normed = row_norm(whole_rows.astype(jnp.float32), gain_rotated).astype(jnp.bfloat16)
        projected = jnp.dot(normed, proj_rotated, preferred_element_type=jnp.float32)
        partial_value, state_new, conv_new = mix_channels(
            projected.reshape(doc_count, length, -1),
            conv_start,
            state_start,
            conv_weight[0],
            conv_bias[0],
            step_bias[0],
            decay_rate[0],
            skip_gain[0],
            gate_gain[0],
            out_proj[0],
        )
        result = scatter_sum(partial_value, weight_blocks, current.astype(jnp.float32)).astype(jnp.bfloat16)
        results = (result, state_new, conv_new)
        incoming = result
    out_rows, new_states, new_convs = results
    return (out_rows[None], new_states[None], new_convs[None])


def solution(mesh):
    in_specs = (
        P("dp", "mp"),
        P("section", None),
        P("section", None, "mp"),
        P("section", None, "mp"),
        P("section", "mp"),
        P("section", "mp"),
        P("section", "mp"),
        P("section", "mp"),
        P("section", "mp"),
        P("section", "mp", None),
        P("section", "dp", "mp", None),
        P("section", "dp", None, "mp"),
        P(),
        P(),
        P("dp"),
    )
    out_specs = (
        P("section", "dp", "mp"),
        P("section", "dp", "mp", None),
        P("section", "dp", None, "mp"),
    )
    return jax.shard_map(
        per_device, mesh=mesh, in_specs=in_specs, out_specs=out_specs, check_vma=False
    )
```

```python
import jax
import jax.numpy as jnp
from jax import lax
from jax.sharding import PartitionSpec as P

epsilon = 1e-05
highest = lax.Precision.HIGHEST
three_pass = lax.Precision.HIGH
one_pass = lax.Precision.DEFAULT


def from_behind(value, axis, steps):
    count = lax.axis_size(axis)
    first, last = (max(0, -steps), min(count, count - steps))
    return lax.ppermute(value, axis, [(source, source + steps) for source in range(first, last)])


def row_norm(values, norm_scale):
    inv_rms = lax.rsqrt(jnp.mean(values * values, axis=-1, keepdims=True) + epsilon)
    return values * inv_rms * norm_scale


def mix_channels(
    projected,
    conv_prev,
    state_prev,
    conv_kernel,
    conv_shift,
    step_shift,
    decay_speed,
    skip_weight,
    norm_scale,
    out_weight,
):
    doc_count = projected.shape[0]
    length = projected.shape[1]
    inner = norm_scale.shape[0]
    head_count = decay_speed.shape[0]
    head_dim = inner // head_count
    state_width = (projected.shape[2] - 2 * inner - head_count) // 2
    kernel_len = conv_kernel.shape[0]
    gate_cols = projected[:, :, :inner]
    mixed_in = projected[:, :, inner : 2 * inner + 2 * state_width]
    step_raw = projected[:, :, 2 * inner + 2 * state_width :]
    padded = jnp.concatenate([conv_prev, mixed_in], axis=1)
    conv_out = jnp.zeros_like(mixed_in) + conv_shift
    for offset in range(kernel_len):
        conv_out = conv_out + conv_kernel[offset] * padded[:, offset : offset + length]
    activated = jax.nn.silu(conv_out)
    chan_vals = activated[:, :, :inner]
    expander = (
        jnp.arange(inner)[None, :] // head_dim == jnp.arange(head_count)[:, None]
    ).astype(jnp.float32)

    def expand(per_head):
        return jnp.einsum("...h,hm->...m", per_head, expander, precision=highest)

    key_proj = activated[:, :, inner : inner + state_width]
    query_proj = activated[:, :, inner + state_width :]
    step_size = jax.nn.softplus(step_raw + step_shift)
    cum_decay = jnp.cumsum(-step_size * decay_speed, axis=1)
    pair_decay = cum_decay[:, :, None, :] - cum_decay[:, None, :, :]
    positions = jnp.arange(length)
    causal = positions[:, None] >= positions[None, :]
    decay = jnp.exp(jnp.where(causal[None, :, :, None], pair_decay, -1e30))
    scores = jnp.einsum("dtn,dsn->dts", query_proj, key_proj, precision=three_pass)
    weights = decay * scores[:, :, :, None] * step_size[:, None, :, :]
    spread = chan_vals[:, :, None, :] * expander[None, None, :, :]
    mixed_out = jnp.einsum("dtsh,dshm->dtm", weights, spread, precision=one_pass)
    start_state = state_prev.reshape(doc_count, inner, state_width).astype(jnp.float32)
    carried = jnp.einsum("dtn,dmn->dtm", query_proj, start_state, precision=one_pass)
    mixed_out = mixed_out + expand(jnp.exp(cum_decay)) * carried
    mixed_out = mixed_out + jnp.repeat(skip_weight, head_dim)[None, None, :] * chan_vals
    tail_weight = jnp.exp(cum_decay[:, -1:, :] - cum_decay) * step_size
    scaled_vals = expand(tail_weight) * chan_vals
    end_state = expand(jnp.exp(cum_decay[:, -1, :]))[:, :, None] * start_state
    end_state = end_state + jnp.einsum("dsm,dsn->dmn", scaled_vals, key_proj, precision=three_pass)
    new_conv = mixed_in[:, length - (kernel_len - 1) :].astype(jnp.bfloat16)
    gated = mixed_out * jax.nn.silu(gate_cols)
    gnormed = row_norm(gated, norm_scale).astype(jnp.bfloat16)
    partial_value = gnormed.reshape(doc_count * length, inner)
    end_rounded = end_state.reshape(doc_count, head_count, head_dim * state_width).astype(
        jnp.bfloat16
    )
    return (partial_value, end_rounded, new_conv)


def shifted(value, axis, steps):
    count = lax.axis_size(axis)
    return lax.ppermute(value, axis, [(source, (source + steps) % count) for source in range(count)])


def gather_columns(value):
    count = lax.axis_size("mp")
    parts = [value] + [shifted(value, "mp", steps) for steps in range(1, count)]
    return jnp.concatenate(parts[::-1], axis=1)


def rotate_rows(value, block):
    count = lax.axis_size("mp")
    position = lax.axis_index("mp")
    doubled = jnp.concatenate([value, value], axis=0)
    return lax.dynamic_slice_in_dim(doubled, ((position + 1) % count) * block, count * block, 0)


def gather_from_behind(value):
    count = lax.axis_size("mp")
    sections = lax.axis_size("section")
    width = value.shape[1]
    position = lax.axis_index("mp")
    parts = []
    for steps in range(count):
        pairs = [
            (section * count + source, (section + 1) * count + (source + steps) % count)
            for section in range(sections - 1)
            for source in range(count)
        ]
        parts.append(lax.ppermute(value, ("section", "mp"), pairs))
    whole = jnp.concatenate(parts[::-1], axis=1)
    return whole, parts[0]


def column_blocks(out_weight):
    count = lax.axis_size("mp")
    position = lax.axis_index("mp")
    width = out_weight.shape[1] // count
    return [
        lax.dynamic_slice_in_dim(out_weight, ((position + steps) % count) * width, width, 1)
        for steps in range(count)
    ]


def scatter_sum(gnormed, weight_blocks, base):
    total = base
    for steps, weight_block in enumerate(weight_blocks):
        block = jnp.dot(gnormed, weight_block, preferred_element_type=jnp.float32).astype(jnp.bfloat16)
        if steps > 0:
            block = shifted(block, "mp", steps)
        total = total + block.astype(jnp.float32)
    return total


def per_device(
    tokens,
    norm_gain,
    in_proj,
    conv_weight,
    conv_bias,
    step_bias,
    decay_rate,
    skip_gain,
    gate_gain,
    out_proj,
    kept_state,
    kept_conv,
    doc_owner,
    doc_slot,
    window_start,
):
    dp_count = lax.axis_size("dp")
    section_count = lax.axis_size("section")
    dp_idx = lax.axis_index("dp")
    section_idx = lax.axis_index("section")
    doc_count = window_start.shape[0]
    length = tokens.shape[0] // doc_count
    shard_width = tokens.shape[1]
    capacity = (doc_count + dp_count - 1) // dp_count
    owners = doc_owner.reshape(dp_count, doc_count)
    slots = doc_slot.reshape(dp_count, doc_count)
    positions = jnp.arange(doc_count)
    earlier = positions[:, None] > positions[None, :]
    same_owner = owners[:, :, None] == owners[:, None, :]
    owner_rank = jnp.sum(jnp.logical_and(same_owner, earlier[None]), axis=2)
    chosen = jnp.logical_and(
        (owners == dp_idx)[:, :, None],
        owner_rank[:, :, None] == jnp.arange(capacity)[None, None, :],
    )
    send_index = jnp.sum(jnp.where(chosen, slots[:, :, None], 0), axis=1).reshape(-1)
    heads_dev = kept_state.shape[2]
    state_cols = kept_state.shape[3]
    chans = conv_weight.shape[2]
    kernel_len = conv_weight.shape[1]
    slot_count = kept_state.shape[1]
    send_pick = (send_index[:, None] == jnp.arange(slot_count)[None, :]).astype(jnp.bfloat16)

    def select_rows(picker, rows):
        picked = jnp.dot(picker, rows.reshape(rows.shape[0], -1), preferred_element_type=jnp.float32)
        return picked.astype(jnp.bfloat16).reshape((picker.shape[0],) + rows.shape[1:])

    send_state = select_rows(send_pick, kept_state[0])
    send_conv = select_rows(send_pick, kept_conv[0])
    got_conv = lax.all_to_all(send_conv, "dp", split_axis=0, concat_axis=0, tiled=True)
    got_state = lax.all_to_all(send_state, "dp", split_axis=0, concat_axis=0, tiled=True)
    my_owners = lax.dynamic_index_in_dim(owners, dp_idx, 0, keepdims=False)
    my_rank = lax.dynamic_index_in_dim(owner_rank, dp_idx, 0, keepdims=False)
    recv_row = my_owners * capacity + my_rank
    keep_flag = (window_start > 0).astype(jnp.float32)
    recv_pick = (recv_row[:, None] == jnp.arange(got_state.shape[0])[None, :]).astype(jnp.float32)
    recv_pick = (recv_pick * keep_flag[:, None]).astype(jnp.bfloat16)
    state_start = select_rows(recv_pick, got_state)
    conv_start = select_rows(recv_pick, got_conv).astype(jnp.float32)
    gain_rotated = rotate_rows(norm_gain[0], shard_width)
    proj_rotated = rotate_rows(in_proj[0], shard_width)
    weight_blocks = column_blocks(out_proj[0])
    results = None
    incoming = None
    first_rows = None
    for phase in range(section_count):
        if incoming is None:
            current = tokens
            whole_rows = gather_columns(current)
            first_rows = whole_rows
        else:
            gathered, incoming = gather_from_behind(result)
            current = jnp.where(section_idx == 0, tokens, incoming)
            whole_rows = jnp.where(section_idx == 0, first_rows, gathered)
        normed = row_norm(whole_rows.astype(jnp.float32), gain_rotated).astype(jnp.bfloat16)
        projected = jnp.dot(normed, proj_rotated, preferred_element_type=jnp.float32)
        partial_value, state_new, conv_new = mix_channels(
            projected.reshape(doc_count, length, -1),
            conv_start,
            state_start,
            conv_weight[0],
            conv_bias[0],
            step_bias[0],
            decay_rate[0],
            skip_gain[0],
            gate_gain[0],
            out_proj[0],
        )
        result = scatter_sum(partial_value, weight_blocks, current.astype(jnp.float32)).astype(jnp.bfloat16)
        results = (result, state_new, conv_new)
        incoming = result
    out_rows, new_states, new_convs = results
    return (out_rows[None], new_states[None], new_convs[None])


def solution(mesh):
    in_specs = (
        P("dp", "mp"),
        P("section", None),
        P("section", None, "mp"),
        P("section", None, "mp"),
        P("section", "mp"),
        P("section", "mp"),
        P("section", "mp"),
        P("section", "mp"),
        P("section", "mp"),
        P("section", "mp", None),
        P("section", "dp", "mp", None),
        P("section", "dp", None, "mp"),
        P(),
        P(),
        P("dp"),
    )
    out_specs = (
        P("section", "dp", "mp"),
        P("section", "dp", "mp", None),
        P("section", "dp", None, "mp"),
    )
    return jax.shard_map(
        per_device, mesh=mesh, in_specs=in_specs, out_specs=out_specs, check_vma=False
    )
```

```python
import jax
import jax.numpy as jnp
from jax import lax
from jax.sharding import PartitionSpec as P

epsilon = 1e-05
highest = lax.Precision.HIGHEST
three_pass = lax.Precision.HIGH
one_pass = lax.Precision.DEFAULT


def from_behind(value, axis, steps):
    count = lax.axis_size(axis)
    first, last = (max(0, -steps), min(count, count - steps))
    return lax.ppermute(value, axis, [(source, source + steps) for source in range(first, last)])


def row_norm(values, norm_scale):
    inv_rms = lax.rsqrt(jnp.mean(values * values, axis=-1, keepdims=True) + epsilon)
    return values * inv_rms * norm_scale


def mix_channels(
    projected,
    conv_prev,
    state_prev,
    conv_kernel,
    conv_shift,
    step_shift,
    decay_speed,
    skip_weight,
    norm_scale,
    out_weight,
):
    doc_count = projected.shape[0]
    length = projected.shape[1]
    inner = norm_scale.shape[0]
    head_count = decay_speed.shape[0]
    head_dim = inner // head_count
    state_width = (projected.shape[2] - 2 * inner - head_count) // 2
    kernel_len = conv_kernel.shape[0]
    gate_cols = projected[:, :, :inner]
    mixed_in = projected[:, :, inner : 2 * inner + 2 * state_width]
    step_raw = projected[:, :, 2 * inner + 2 * state_width :]
    padded = jnp.concatenate([conv_prev, mixed_in], axis=1)
    conv_out = jnp.zeros_like(mixed_in) + conv_shift
    for offset in range(kernel_len):
        conv_out = conv_out + conv_kernel[offset] * padded[:, offset : offset + length]
    activated = jax.nn.silu(conv_out)
    chan_vals = activated[:, :, :inner]
    expander = (
        jnp.arange(inner)[None, :] // head_dim == jnp.arange(head_count)[:, None]
    ).astype(jnp.float32)

    def expand(per_head):
        return jnp.einsum("...h,hm->...m", per_head, expander, precision=highest)

    key_proj = activated[:, :, inner : inner + state_width]
    query_proj = activated[:, :, inner + state_width :]
    step_size = jax.nn.softplus(step_raw + step_shift)
    cum_decay = jnp.cumsum(-step_size * decay_speed, axis=1)
    pair_decay = cum_decay[:, :, None, :] - cum_decay[:, None, :, :]
    positions = jnp.arange(length)
    causal = positions[:, None] >= positions[None, :]
    decay = jnp.exp(jnp.where(causal[None, :, :, None], pair_decay, -1e30))
    scores = jnp.einsum("dtn,dsn->dts", query_proj, key_proj, precision=three_pass)
    weights = decay * scores[:, :, :, None] * step_size[:, None, :, :]
    spread = chan_vals[:, :, None, :] * expander[None, None, :, :]
    mixed_out = jnp.einsum("dtsh,dshm->dtm", weights, spread, precision=one_pass)
    start_state = state_prev.reshape(doc_count, inner, state_width).astype(jnp.float32)
    carried = jnp.einsum("dtn,dmn->dtm", query_proj, start_state, precision=one_pass)
    mixed_out = mixed_out + expand(jnp.exp(cum_decay)) * carried
    mixed_out = mixed_out + jnp.repeat(skip_weight, head_dim)[None, None, :] * chan_vals
    tail_weight = jnp.exp(cum_decay[:, -1:, :] - cum_decay) * step_size
    scaled_vals = expand(tail_weight) * chan_vals
    end_state = expand(jnp.exp(cum_decay[:, -1, :]))[:, :, None] * start_state
    end_state = end_state + jnp.einsum("dsm,dsn->dmn", scaled_vals, key_proj, precision=three_pass)
    new_conv = mixed_in[:, length - (kernel_len - 1) :].astype(jnp.bfloat16)
    gated = mixed_out * jax.nn.silu(gate_cols)
    gnormed = row_norm(gated, norm_scale).astype(jnp.bfloat16)
    partial_value = gnormed.reshape(doc_count * length, inner)
    end_rounded = end_state.reshape(doc_count, head_count, head_dim * state_width).astype(
        jnp.bfloat16
    )
    return (partial_value, end_rounded, new_conv)


def shifted(value, axis, steps):
    count = lax.axis_size(axis)
    return lax.ppermute(value, axis, [(source, (source + steps) % count) for source in range(count)])


def gather_columns(value):
    count = lax.axis_size("mp")
    parts = [value] + [shifted(value, "mp", steps) for steps in range(1, count)]
    return jnp.concatenate(parts[::-1], axis=1)


def rotate_rows(value, block):
    count = lax.axis_size("mp")
    position = lax.axis_index("mp")
    doubled = jnp.concatenate([value, value], axis=0)
    return lax.dynamic_slice_in_dim(doubled, ((position + 1) % count) * block, count * block, 0)


def gather_from_behind(value):
    count = lax.axis_size("mp")
    sections = lax.axis_size("section")
    width = value.shape[1]
    position = lax.axis_index("mp")
    parts = []
    for steps in range(count):
        pairs = [
            (section * count + source, (section + 1) * count + (source + steps) % count)
            for section in range(sections - 1)
            for source in range(count)
        ]
        parts.append(lax.ppermute(value, ("section", "mp"), pairs))
    whole = jnp.concatenate(parts[::-1], axis=1)
    return whole, parts[0]


def column_blocks(out_weight):
    count = lax.axis_size("mp")
    position = lax.axis_index("mp")
    width = out_weight.shape[1] // count
    return [
        lax.dynamic_slice_in_dim(out_weight, ((position + steps) % count) * width, width, 1)
        for steps in range(count)
    ]


def scatter_sum(gnormed, weight_blocks, base):
    total = base
    for steps, weight_block in enumerate(weight_blocks):
        block = jnp.dot(gnormed, weight_block, preferred_element_type=jnp.float32).astype(jnp.bfloat16)
        if steps > 0:
            block = shifted(block, "mp", steps)
        total = total + block.astype(jnp.float32)
    return total


def per_device(
    tokens,
    norm_gain,
    in_proj,
    conv_weight,
    conv_bias,
    step_bias,
    decay_rate,
    skip_gain,
    gate_gain,
    out_proj,
    kept_state,
    kept_conv,
    doc_owner,
    doc_slot,
    window_start,
):
    dp_count = lax.axis_size("dp")
    section_count = lax.axis_size("section")
    dp_idx = lax.axis_index("dp")
    section_idx = lax.axis_index("section")
    doc_count = window_start.shape[0]
    length = tokens.shape[0] // doc_count
    shard_width = tokens.shape[1]
    capacity = (doc_count + dp_count - 1) // dp_count
    owners = doc_owner.reshape(dp_count, doc_count)
    slots = doc_slot.reshape(dp_count, doc_count)
    positions = jnp.arange(doc_count)
    earlier = positions[:, None] > positions[None, :]
    same_owner = owners[:, :, None] == owners[:, None, :]
    owner_rank = jnp.sum(jnp.logical_and(same_owner, earlier[None]), axis=2)
    chosen = jnp.logical_and(
        (owners == dp_idx)[:, :, None],
        owner_rank[:, :, None] == jnp.arange(capacity)[None, None, :],
    )
    send_index = jnp.sum(jnp.where(chosen, slots[:, :, None], 0), axis=1).reshape(-1)
    heads_dev = kept_state.shape[2]
    state_cols = kept_state.shape[3]
    chans = conv_weight.shape[2]
    kernel_len = conv_weight.shape[1]
    slot_count = kept_state.shape[1]
    send_pick = (send_index[:, None] == jnp.arange(slot_count)[None, :]).astype(jnp.bfloat16)

    def select_rows(picker, rows):
        picked = jnp.dot(picker, rows.reshape(rows.shape[0], -1), preferred_element_type=jnp.float32)
        return picked.astype(jnp.bfloat16).reshape((picker.shape[0],) + rows.shape[1:])

    send_state = select_rows(send_pick, kept_state[0])
    got_state = lax.all_to_all(send_state, "dp", split_axis=0, concat_axis=0, tiled=True)
    by_shift = (jnp.arange(dp_count) + dp_idx) % dp_count
    shift_order = jnp.take(send_index.reshape(dp_count, capacity), by_shift, axis=0).reshape(-1)
    shift_pick = (shift_order[:, None] == jnp.arange(slot_count)[None, :]).astype(jnp.bfloat16)
    send_conv = select_rows(shift_pick, kept_conv[0])
    conv_chunks = [send_conv[:capacity]]
    for steps in range(1, dp_count):
        conv_chunks.append(shifted(send_conv[steps * capacity : (steps + 1) * capacity], "dp", steps))
    got_conv = jnp.concatenate(conv_chunks, axis=0)
    my_owners = lax.dynamic_index_in_dim(owners, dp_idx, 0, keepdims=False)
    my_rank = lax.dynamic_index_in_dim(owner_rank, dp_idx, 0, keepdims=False)
    keep_flag = (window_start > 0).astype(jnp.float32)

    def receive_pick(rows_at):
        picker = (rows_at[:, None] == jnp.arange(got_state.shape[0])[None, :]).astype(jnp.float32)
        return (picker * keep_flag[:, None]).astype(jnp.bfloat16)

    state_start = select_rows(receive_pick(my_owners * capacity + my_rank), got_state)
    shift_rows = ((dp_idx - my_owners) % dp_count) * capacity + my_rank
    conv_start = select_rows(receive_pick(shift_rows), got_conv).astype(jnp.float32)
    gain_rotated = rotate_rows(norm_gain[0], shard_width)
    proj_rotated = rotate_rows(in_proj[0], shard_width)
    weight_blocks = column_blocks(out_proj[0])
    results = None
    incoming = None
    first_rows = None
    for phase in range(section_count):
        if incoming is None:
            current = tokens
            whole_rows = gather_columns(current)
            first_rows = whole_rows
        else:
            gathered, incoming = gather_from_behind(result)
            current = jnp.where(section_idx == 0, tokens, incoming)
            whole_rows = jnp.where(section_idx == 0, first_rows, gathered)
        normed = row_norm(whole_rows.astype(jnp.float32), gain_rotated).astype(jnp.bfloat16)
        projected = jnp.dot(normed, proj_rotated, preferred_element_type=jnp.float32)
        partial_value, state_new, conv_new = mix_channels(
            projected.reshape(doc_count, length, -1),
            conv_start,
            state_start,
            conv_weight[0],
            conv_bias[0],
            step_bias[0],
            decay_rate[0],
            skip_gain[0],
            gate_gain[0],
            out_proj[0],
        )
        result = scatter_sum(partial_value, weight_blocks, current.astype(jnp.float32)).astype(jnp.bfloat16)
        results = (result, state_new, conv_new)
        incoming = result
    out_rows, new_states, new_convs = results
    return (out_rows[None], new_states[None], new_convs[None])


def solution(mesh):
    in_specs = (
        P("dp", "mp"),
        P("section", None),
        P("section", None, "mp"),
        P("section", None, "mp"),
        P("section", "mp"),
        P("section", "mp"),
        P("section", "mp"),
        P("section", "mp"),
        P("section", "mp"),
        P("section", "mp", None),
        P("section", "dp", "mp", None),
        P("section", "dp", None, "mp"),
        P(),
        P(),
        P("dp"),
    )
    out_specs = (
        P("section", "dp", "mp"),
        P("section", "dp", "mp", None),
        P("section", "dp", None, "mp"),
    )
    return jax.shard_map(
        per_device, mesh=mesh, in_specs=in_specs, out_specs=out_specs, check_vma=False
    )
```

```python
import jax
import jax.numpy as jnp
from jax import lax
from jax.sharding import PartitionSpec as P

epsilon = 1e-05
highest = lax.Precision.HIGHEST
three_pass = lax.Precision.HIGH
one_pass = lax.Precision.DEFAULT


def from_behind(value, axis, steps):
    count = lax.axis_size(axis)
    first, last = (max(0, -steps), min(count, count - steps))
    return lax.ppermute(value, axis, [(source, source + steps) for source in range(first, last)])


def row_norm(values, norm_scale):
    inv_rms = lax.rsqrt(jnp.mean(values * values, axis=-1, keepdims=True) + epsilon)
    return values * inv_rms * norm_scale


def mix_channels(
    projected,
    conv_prev,
    state_prev,
    conv_kernel,
    conv_shift,
    step_shift,
    decay_speed,
    skip_weight,
    norm_scale,
    out_weight,
):
    doc_count = projected.shape[0]
    length = projected.shape[1]
    inner = norm_scale.shape[0]
    head_count = decay_speed.shape[0]
    head_dim = inner // head_count
    state_width = (projected.shape[2] - 2 * inner - head_count) // 2
    kernel_len = conv_kernel.shape[0]
    gate_cols = projected[:, :, :inner]
    mixed_in = projected[:, :, inner : 2 * inner + 2 * state_width]
    step_raw = projected[:, :, 2 * inner + 2 * state_width :]
    padded = jnp.concatenate([conv_prev, mixed_in], axis=1)
    conv_out = jnp.zeros_like(mixed_in) + conv_shift
    for offset in range(kernel_len):
        conv_out = conv_out + conv_kernel[offset] * padded[:, offset : offset + length]
    activated = jax.nn.silu(conv_out)
    chan_vals = activated[:, :, :inner]
    expander = (
        jnp.arange(inner)[None, :] // head_dim == jnp.arange(head_count)[:, None]
    ).astype(jnp.float32)

    def expand(per_head):
        return jnp.einsum("...h,hm->...m", per_head, expander, precision=highest)

    key_proj = activated[:, :, inner : inner + state_width]
    query_proj = activated[:, :, inner + state_width :]
    step_size = jax.nn.softplus(step_raw + step_shift)
    cum_decay = jnp.cumsum(-step_size * decay_speed, axis=1)
    pair_decay = cum_decay[:, :, None, :] - cum_decay[:, None, :, :]
    positions = jnp.arange(length)
    causal = positions[:, None] >= positions[None, :]
    decay = jnp.exp(jnp.where(causal[None, :, :, None], pair_decay, -1e30))
    scores = jnp.einsum("dtn,dsn->dts", query_proj, key_proj, precision=three_pass)
    weights = decay * scores[:, :, :, None] * step_size[:, None, :, :]
    spread = chan_vals[:, :, None, :] * expander[None, None, :, :]
    mixed_out = jnp.einsum("dtsh,dshm->dtm", weights, spread, precision=one_pass)
    start_state = state_prev.reshape(doc_count, inner, state_width).astype(jnp.float32)
    carried = jnp.einsum("dtn,dmn->dtm", query_proj, start_state, precision=one_pass)
    mixed_out = mixed_out + expand(jnp.exp(cum_decay)) * carried
    mixed_out = mixed_out + jnp.repeat(skip_weight, head_dim)[None, None, :] * chan_vals
    tail_weight = jnp.exp(cum_decay[:, -1:, :] - cum_decay) * step_size
    scaled_vals = expand(tail_weight) * chan_vals
    end_state = expand(jnp.exp(cum_decay[:, -1, :]))[:, :, None] * start_state
    end_state = end_state + jnp.einsum("dsm,dsn->dmn", scaled_vals, key_proj, precision=three_pass)
    new_conv = mixed_in[:, length - (kernel_len - 1) :].astype(jnp.bfloat16)
    gated = mixed_out * jax.nn.silu(gate_cols)
    gnormed = row_norm(gated, norm_scale).astype(jnp.bfloat16)
    partial_value = gnormed.reshape(doc_count * length, inner)
    end_rounded = end_state.reshape(doc_count, head_count, head_dim * state_width).astype(
        jnp.bfloat16
    )
    return (partial_value, end_rounded, new_conv)


def shifted(value, axis, steps):
    count = lax.axis_size(axis)
    return lax.ppermute(value, axis, [(source, (source + steps) % count) for source in range(count)])


def gather_columns(value):
    count = lax.axis_size("mp")
    parts = [value] + [shifted(value, "mp", steps) for steps in range(1, count)]
    return jnp.concatenate(parts[::-1], axis=1)


def rotate_rows(value, block):
    count = lax.axis_size("mp")
    position = lax.axis_index("mp")
    doubled = jnp.concatenate([value, value], axis=0)
    return lax.dynamic_slice_in_dim(doubled, ((position + 1) % count) * block, count * block, 0)


def gather_from_behind(value):
    count = lax.axis_size("mp")
    sections = lax.axis_size("section")
    width = value.shape[1]
    position = lax.axis_index("mp")
    parts = []
    for steps in range(count):
        pairs = [
            (section * count + source, (section + 1) * count + (source + steps) % count)
            for section in range(sections - 1)
            for source in range(count)
        ]
        parts.append(lax.ppermute(value, ("section", "mp"), pairs))
    whole = jnp.concatenate(parts[::-1], axis=1)
    return whole, parts[0]


def column_blocks(out_weight):
    count = lax.axis_size("mp")
    position = lax.axis_index("mp")
    width = out_weight.shape[1] // count
    return [
        lax.dynamic_slice_in_dim(out_weight, ((position + steps) % count) * width, width, 1)
        for steps in range(count)
    ]


def scatter_sum(gnormed, weight_blocks, base):
    total = base
    for steps, weight_block in enumerate(weight_blocks):
        block = jnp.dot(gnormed, weight_block, preferred_element_type=jnp.float32).astype(jnp.bfloat16)
        if steps > 0:
            block = shifted(block, "mp", steps)
        total = total + block.astype(jnp.float32)
    return total


def per_device(
    tokens,
    norm_gain,
    in_proj,
    conv_weight,
    conv_bias,
    step_bias,
    decay_rate,
    skip_gain,
    gate_gain,
    out_proj,
    kept_state,
    kept_conv,
    doc_owner,
    doc_slot,
    window_start,
):
    dp_count = lax.axis_size("dp")
    section_count = lax.axis_size("section")
    dp_idx = lax.axis_index("dp")
    section_idx = lax.axis_index("section")
    doc_count = window_start.shape[0]
    length = tokens.shape[0] // doc_count
    shard_width = tokens.shape[1]
    capacity = (doc_count + dp_count - 1) // dp_count
    owners = doc_owner.reshape(dp_count, doc_count)
    slots = doc_slot.reshape(dp_count, doc_count)
    positions = jnp.arange(doc_count)
    earlier = positions[:, None] > positions[None, :]
    same_owner = owners[:, :, None] == owners[:, None, :]
    owner_rank = jnp.sum(jnp.logical_and(same_owner, earlier[None]), axis=2)
    chosen = jnp.logical_and(
        (owners == dp_idx)[:, :, None],
        owner_rank[:, :, None] == jnp.arange(capacity)[None, None, :],
    )
    send_index = jnp.sum(jnp.where(chosen, slots[:, :, None], 0), axis=1).reshape(-1)
    heads_dev = kept_state.shape[2]
    state_cols = kept_state.shape[3]
    chans = conv_weight.shape[2]
    kernel_len = conv_weight.shape[1]
    slot_count = kept_state.shape[1]
    send_pick = (send_index[:, None] == jnp.arange(slot_count)[None, :]).astype(jnp.bfloat16)

    def select_rows(picker, rows):
        picked = jnp.dot(picker, rows.reshape(rows.shape[0], -1), preferred_element_type=jnp.float32)
        return picked.astype(jnp.bfloat16).reshape((picker.shape[0],) + rows.shape[1:])

    send_state = kept_state[0][send_index]
    got_state = lax.all_to_all(send_state, "dp", split_axis=0, concat_axis=0, tiled=True)
    by_shift = (jnp.arange(dp_count) + dp_idx) % dp_count
    shift_order = jnp.take(send_index.reshape(dp_count, capacity), by_shift, axis=0).reshape(-1)
    shift_pick = (shift_order[:, None] == jnp.arange(slot_count)[None, :]).astype(jnp.bfloat16)
    send_conv = kept_conv[0][shift_order]
    conv_chunks = [send_conv[:capacity]]
    for steps in range(1, dp_count):
        conv_chunks.append(shifted(send_conv[steps * capacity : (steps + 1) * capacity], "dp", steps))
    got_conv = jnp.concatenate(conv_chunks, axis=0)
    my_owners = lax.dynamic_index_in_dim(owners, dp_idx, 0, keepdims=False)
    my_rank = lax.dynamic_index_in_dim(owner_rank, dp_idx, 0, keepdims=False)
    keep_flag = (window_start > 0).astype(jnp.float32)

    def receive_pick(rows_at):
        picker = (rows_at[:, None] == jnp.arange(got_state.shape[0])[None, :]).astype(jnp.float32)
        return (picker * keep_flag[:, None]).astype(jnp.bfloat16)

    state_start = select_rows(receive_pick(my_owners * capacity + my_rank), got_state)
    shift_rows = ((dp_idx - my_owners) % dp_count) * capacity + my_rank
    conv_start = select_rows(receive_pick(shift_rows), got_conv).astype(jnp.float32)
    gain_rotated = rotate_rows(norm_gain[0], shard_width)
    proj_rotated = rotate_rows(in_proj[0], shard_width)
    weight_blocks = column_blocks(out_proj[0])
    results = None
    incoming = None
    first_rows = None
    for phase in range(section_count):
        if incoming is None:
            current = tokens
            whole_rows = gather_columns(current)
            first_rows = whole_rows
        else:
            gathered, incoming = gather_from_behind(result)
            current = jnp.where(section_idx == 0, tokens, incoming)
            whole_rows = jnp.where(section_idx == 0, first_rows, gathered)
        normed = row_norm(whole_rows.astype(jnp.float32), gain_rotated).astype(jnp.bfloat16)
        projected = jnp.dot(normed, proj_rotated, preferred_element_type=jnp.float32)
        partial_value, state_new, conv_new = mix_channels(
            projected.reshape(doc_count, length, -1),
            conv_start,
            state_start,
            conv_weight[0],
            conv_bias[0],
            step_bias[0],
            decay_rate[0],
            skip_gain[0],
            gate_gain[0],
            out_proj[0],
        )
        result = scatter_sum(partial_value, weight_blocks, current.astype(jnp.float32)).astype(jnp.bfloat16)
        results = (result, state_new, conv_new)
        incoming = result
    out_rows, new_states, new_convs = results
    return (out_rows[None], new_states[None], new_convs[None])


def solution(mesh):
    in_specs = (
        P("dp", "mp"),
        P("section", None),
        P("section", None, "mp"),
        P("section", None, "mp"),
        P("section", "mp"),
        P("section", "mp"),
        P("section", "mp"),
        P("section", "mp"),
        P("section", "mp"),
        P("section", "mp", None),
        P("section", "dp", "mp", None),
        P("section", "dp", None, "mp"),
        P(),
        P(),
        P("dp"),
    )
    out_specs = (
        P("section", "dp", "mp"),
        P("section", "dp", "mp", None),
        P("section", "dp", None, "mp"),
    )
    return jax.shard_map(
        per_device, mesh=mesh, in_specs=in_specs, out_specs=out_specs, check_vma=False
    )
```

```python
import jax
import jax.numpy as jnp
from jax import lax
from jax.sharding import PartitionSpec as P

epsilon = 1e-05
highest = lax.Precision.HIGHEST
three_pass = lax.Precision.HIGH
one_pass = lax.Precision.DEFAULT


def from_behind(value, axis, steps):
    count = lax.axis_size(axis)
    first, last = (max(0, -steps), min(count, count - steps))
    return lax.ppermute(value, axis, [(source, source + steps) for source in range(first, last)])


def row_norm(values, norm_scale):
    inv_rms = lax.rsqrt(jnp.mean(values * values, axis=-1, keepdims=True) + epsilon)
    return values * inv_rms * norm_scale


def mix_channels(
    projected,
    conv_prev,
    state_prev,
    conv_kernel,
    conv_shift,
    step_shift,
    decay_speed,
    skip_weight,
    norm_scale,
    out_weight,
):
    doc_count = projected.shape[0]
    length = projected.shape[1]
    inner = norm_scale.shape[0]
    head_count = decay_speed.shape[0]
    head_dim = inner // head_count
    state_width = (projected.shape[2] - 2 * inner - head_count) // 2
    kernel_len = conv_kernel.shape[0]
    gate_cols = projected[:, :, :inner]
    mixed_in = projected[:, :, inner : 2 * inner + 2 * state_width]
    step_raw = projected[:, :, 2 * inner + 2 * state_width :]
    padded = jnp.concatenate([conv_prev, mixed_in], axis=1)
    conv_out = jnp.zeros_like(mixed_in) + conv_shift
    for offset in range(kernel_len):
        conv_out = conv_out + conv_kernel[offset] * padded[:, offset : offset + length]
    activated = jax.nn.silu(conv_out)
    chan_vals = activated[:, :, :inner]
    expander = (
        jnp.arange(inner)[None, :] // head_dim == jnp.arange(head_count)[:, None]
    ).astype(jnp.float32)

    def expand(per_head):
        return jnp.einsum("...h,hm->...m", per_head, expander, precision=three_pass)

    key_proj = activated[:, :, inner : inner + state_width]
    query_proj = activated[:, :, inner + state_width :]
    step_size = jax.nn.softplus(step_raw + step_shift)
    cum_decay = jnp.cumsum(-step_size * decay_speed, axis=1)
    pair_decay = cum_decay[:, :, None, :] - cum_decay[:, None, :, :]
    positions = jnp.arange(length)
    causal = positions[:, None] >= positions[None, :]
    decay = jnp.exp(jnp.where(causal[None, :, :, None], pair_decay, -1e30))
    scores = jnp.einsum("dtn,dsn->dts", query_proj, key_proj, precision=three_pass)
    weights = decay * scores[:, :, :, None] * step_size[:, None, :, :]
    spread = chan_vals[:, :, None, :] * expander[None, None, :, :]
    mixed_out = jnp.einsum("dtsh,dshm->dtm", weights, spread, precision=one_pass)
    start_state = state_prev.reshape(doc_count, inner, state_width).astype(jnp.float32)
    carried = jnp.einsum("dtn,dmn->dtm", query_proj, start_state, precision=one_pass)
    mixed_out = mixed_out + expand(jnp.exp(cum_decay)) * carried
    mixed_out = mixed_out + jnp.repeat(skip_weight, head_dim)[None, None, :] * chan_vals
    tail_weight = jnp.exp(cum_decay[:, -1:, :] - cum_decay) * step_size
    scaled_vals = expand(tail_weight) * chan_vals
    end_state = expand(jnp.exp(cum_decay[:, -1, :]))[:, :, None] * start_state
    end_state = end_state + jnp.einsum("dsm,dsn->dmn", scaled_vals, key_proj, precision=three_pass)
    new_conv = mixed_in[:, length - (kernel_len - 1) :].astype(jnp.bfloat16)
    gated = mixed_out * jax.nn.silu(gate_cols)
    gnormed = row_norm(gated, norm_scale).astype(jnp.bfloat16)
    partial_value = gnormed.reshape(doc_count * length, inner)
    end_rounded = end_state.reshape(doc_count, head_count, head_dim * state_width).astype(
        jnp.bfloat16
    )
    return (partial_value, end_rounded, new_conv)


def shifted(value, axis, steps):
    count = lax.axis_size(axis)
    return lax.ppermute(value, axis, [(source, (source + steps) % count) for source in range(count)])


def gather_columns(value):
    count = lax.axis_size("mp")
    parts = [value] + [shifted(value, "mp", steps) for steps in range(1, count)]
    return jnp.concatenate(parts[::-1], axis=1)


def rotate_rows(value, block):
    count = lax.axis_size("mp")
    position = lax.axis_index("mp")
    doubled = jnp.concatenate([value, value], axis=0)
    return lax.dynamic_slice_in_dim(doubled, ((position + 1) % count) * block, count * block, 0)


def gather_from_behind(value):
    count = lax.axis_size("mp")
    sections = lax.axis_size("section")
    width = value.shape[1]
    position = lax.axis_index("mp")
    parts = []
    for steps in range(count):
        pairs = [
            (section * count + source, (section + 1) * count + (source + steps) % count)
            for section in range(sections - 1)
            for source in range(count)
        ]
        parts.append(lax.ppermute(value, ("section", "mp"), pairs))
    whole = jnp.concatenate(parts[::-1], axis=1)
    return whole, parts[0]


def column_blocks(out_weight):
    count = lax.axis_size("mp")
    position = lax.axis_index("mp")
    width = out_weight.shape[1] // count
    return [
        lax.dynamic_slice_in_dim(out_weight, ((position + steps) % count) * width, width, 1)
        for steps in range(count)
    ]


def scatter_sum(gnormed, weight_blocks, base):
    total = base
    for steps, weight_block in enumerate(weight_blocks):
        block = jnp.dot(gnormed, weight_block, preferred_element_type=jnp.float32).astype(jnp.bfloat16)
        if steps > 0:
            block = shifted(block, "mp", steps)
        total = total + block.astype(jnp.float32)
    return total


def per_device(
    tokens,
    norm_gain,
    in_proj,
    conv_weight,
    conv_bias,
    step_bias,
    decay_rate,
    skip_gain,
    gate_gain,
    out_proj,
    kept_state,
    kept_conv,
    doc_owner,
    doc_slot,
    window_start,
):
    dp_count = lax.axis_size("dp")
    section_count = lax.axis_size("section")
    dp_idx = lax.axis_index("dp")
    section_idx = lax.axis_index("section")
    doc_count = window_start.shape[0]
    length = tokens.shape[0] // doc_count
    shard_width = tokens.shape[1]
    capacity = (doc_count + dp_count - 1) // dp_count
    owners = doc_owner.reshape(dp_count, doc_count)
    slots = doc_slot.reshape(dp_count, doc_count)
    positions = jnp.arange(doc_count)
    earlier = positions[:, None] > positions[None, :]
    same_owner = owners[:, :, None] == owners[:, None, :]
    owner_rank = jnp.sum(jnp.logical_and(same_owner, earlier[None]), axis=2)
    chosen = jnp.logical_and(
        (owners == dp_idx)[:, :, None],
        owner_rank[:, :, None] == jnp.arange(capacity)[None, None, :],
    )
    send_index = jnp.sum(jnp.where(chosen, slots[:, :, None], 0), axis=1).reshape(-1)
    heads_dev = kept_state.shape[2]
    state_cols = kept_state.shape[3]
    chans = conv_weight.shape[2]
    kernel_len = conv_weight.shape[1]
    slot_count = kept_state.shape[1]
    send_pick = (send_index[:, None] == jnp.arange(slot_count)[None, :]).astype(jnp.bfloat16)

    def select_rows(picker, rows):
        picked = jnp.dot(picker, rows.reshape(rows.shape[0], -1), preferred_element_type=jnp.float32)
        return picked.astype(jnp.bfloat16).reshape((picker.shape[0],) + rows.shape[1:])

    send_state = kept_state[0][send_index]
    got_state = lax.all_to_all(send_state, "dp", split_axis=0, concat_axis=0, tiled=True)
    by_shift = (jnp.arange(dp_count) + dp_idx) % dp_count
    shift_order = jnp.take(send_index.reshape(dp_count, capacity), by_shift, axis=0).reshape(-1)
    shift_pick = (shift_order[:, None] == jnp.arange(slot_count)[None, :]).astype(jnp.bfloat16)
    send_conv = kept_conv[0][shift_order]
    conv_chunks = [send_conv[:capacity]]
    for steps in range(1, dp_count):
        conv_chunks.append(shifted(send_conv[steps * capacity : (steps + 1) * capacity], "dp", steps))
    got_conv = jnp.concatenate(conv_chunks, axis=0)
    my_owners = lax.dynamic_index_in_dim(owners, dp_idx, 0, keepdims=False)
    my_rank = lax.dynamic_index_in_dim(owner_rank, dp_idx, 0, keepdims=False)
    keep_flag = (window_start > 0).astype(jnp.float32)

    def receive_pick(rows_at):
        picker = (rows_at[:, None] == jnp.arange(got_state.shape[0])[None, :]).astype(jnp.float32)
        return (picker * keep_flag[:, None]).astype(jnp.bfloat16)

    state_start = select_rows(receive_pick(my_owners * capacity + my_rank), got_state)
    shift_rows = ((dp_idx - my_owners) % dp_count) * capacity + my_rank
    conv_start = select_rows(receive_pick(shift_rows), got_conv).astype(jnp.float32)
    gain_rotated = rotate_rows(norm_gain[0], shard_width)
    proj_rotated = rotate_rows(in_proj[0], shard_width)
    weight_blocks = column_blocks(out_proj[0])
    results = None
    incoming = None
    first_rows = None
    for phase in range(section_count):
        if incoming is None:
            current = tokens
            whole_rows = gather_columns(current)
            first_rows = whole_rows
        else:
            gathered, incoming = gather_from_behind(result)
            current = jnp.where(section_idx == 0, tokens, incoming)
            whole_rows = jnp.where(section_idx == 0, first_rows, gathered)
        normed = row_norm(whole_rows.astype(jnp.float32), gain_rotated).astype(jnp.bfloat16)
        projected = jnp.dot(normed, proj_rotated, preferred_element_type=jnp.float32)
        partial_value, state_new, conv_new = mix_channels(
            projected.reshape(doc_count, length, -1),
            conv_start,
            state_start,
            conv_weight[0],
            conv_bias[0],
            step_bias[0],
            decay_rate[0],
            skip_gain[0],
            gate_gain[0],
            out_proj[0],
        )
        result = scatter_sum(partial_value, weight_blocks, current.astype(jnp.float32)).astype(jnp.bfloat16)
        results = (result, state_new, conv_new)
        incoming = result
    out_rows, new_states, new_convs = results
    return (out_rows[None], new_states[None], new_convs[None])


def solution(mesh):
    in_specs = (
        P("dp", "mp"),
        P("section", None),
        P("section", None, "mp"),
        P("section", None, "mp"),
        P("section", "mp"),
        P("section", "mp"),
        P("section", "mp"),
        P("section", "mp"),
        P("section", "mp"),
        P("section", "mp", None),
        P("section", "dp", "mp", None),
        P("section", "dp", None, "mp"),
        P(),
        P(),
        P("dp"),
    )
    out_specs = (
        P("section", "dp", "mp"),
        P("section", "dp", "mp", None),
        P("section", "dp", None, "mp"),
    )
    return jax.shard_map(
        per_device, mesh=mesh, in_specs=in_specs, out_specs=out_specs, check_vma=False
    )
```
